512 devices in a mesh: gx: 32 (over y, x), az: 8 (over z), row: 2 (over core).
Axes of the slice: x: 4, y: 8, z: 8, core: 2. Of those that a mesh axis runs over, the one named last changes fastest.
Arguments:
- adjoint: float32 [5, 256, 32, 1024], P(None, 'gx', 'row', 'az'), may hold values from -6 to 6
- coeff: float32 [3, 256, 32, 1024], P(None, 'gx', 'row', 'az'), may hold values from 0.5 to 2
- flux: float32 [3, 5, 5], replicated, may hold values from -1.5 to 1.5
- target_cell: int32 [131072], P(('gx', 'az', 'row')), may hold values from 0 to 16383
- donor_owner: int32 [131072, 1], P(('gx', 'az', 'row')), may hold values from 0 to 31; in each aligned block of 256 rows (0 to 255, 256 to 511, ...) at most 32 rows name the same one
- donor_cell: int32 [131072], P(('gx', 'az', 'row')), may hold values from 0 to 16383
Outputs:
- gradient: float32 [5, 256, 32, 1024], P(None, 'gx', 'row', 'az')
The draws below stay inside these ranges and needn't reach their ends.
Inputs may be any that keep to these rules, and one draw needn't show every extreme that they name: Each target point's donor lies on the slab donor_owner names; among the 256 target points of one device at most 32 name the same owner, and 32 is reached in every draw. `target_cell`: A flattened cell index inside one device's block. `donor_cell`: A flattened cell index inside the owner's block.
All inputs are finite; a program needn't handle non-finite values.
Results may differ from the reference program's by a relative error of at most 0.0003.
Values sent between devices are 32-bit elements; how exact they have to be, the bound alone decides.
No kernel may reach another device: no remote copies, remote signals or barrier semaphores. Data moves between devices by JAX's collectives and lax.ppermute only.
A program may use at most 64 MiB of HBM per device.

```python
import math
import jax
import jax.numpy as jnp
import numpy as np
from jax import lax

F = 5
CX = 8
CR = 16
CA = 128
TGT = 256
CAP = 32
NX = 256
NR = 32
NA = 1024
TARGETS = 131072
N_GX = 32
N_AZ = 8
N_ROW = 2


def touch_ends(entries, rng, least, largest):
    place = [jax.random.randint(jax.random.fold_in(rng, axis), (), 0, length) for axis, length in enumerate(entries.shape)]
    widest = entries.shape.index(max(entries.shape))
    beside = place[:widest] + [(place[widest] + 1) % entries.shape[widest]] + place[widest + 1:]
    return entries.at[tuple(place)].set(least).at[tuple(beside)].set(largest)


def levels(rng, extent, split, low, largest):
    level = 1.0
    for axis_at, shards_of in split:
        steps = jax.random.uniform(jax.random.fold_in(jax.random.fold_in(rng, 6), axis_at), (shards_of,), jnp.float32, low / len(split), largest / len(split))
        level = level * jnp.repeat(jnp.exp(steps), extent[axis_at] // shards_of).reshape((-1,) + (1,) * (len(extent) - 1 - axis_at))
    return level


def assign_block(key, own, number, rows, number_of, top, reach, skew):
    order = jax.random.permutation(key, number_of)
    packed, usual = portions_of(number_of, rows * top, reach, skew, True), portions_of(number_of, rows * top, reach, skew, False)
    places = jnp.arange(number_of)

    def named(lengths, rotation):
        used = int((lengths > 0).sum())
        fixed = max(1, used // 4)
        moved = fixed + (places - fixed + rotation * (used - fixed)) % max(1, number_of - fixed)
        return jnp.zeros((number_of,), jnp.int32).at[order[jnp.where(places < fixed, places, moved)]].set(jnp.asarray(lengths, jnp.int32))

    lengths = jnp.where(number % 4 == 0, named(packed, number // 4), named(usual, number - number // 4 - 1))
    mixed = jax.random.permutation(jax.random.fold_in(own, 3), number_of)
    giver, sink = mixed[0:number_of // 2 * 2:2], mixed[1:number_of // 2 * 2:2]
    margin = jnp.minimum(lengths[giver] - 1, reach - lengths[sink]) // 2
    margin = jnp.where((giver == order[0]) | (sink == order[0]) | (lengths[sink] == 0), 0, jnp.maximum(margin, 0))
    moved = jax.random.randint(jax.random.fold_in(own, 4), (number_of // 2,), 0, 1 << 20) % (margin + 1)
    lengths = lengths.at[giver].add(-moved).at[sink].add(moved)
    items = jnp.searchsorted(jnp.cumsum(lengths), jnp.arange(rows * top), side="right").astype(jnp.int32)
    grid = items.reshape(top, rows).T
    grid = grid[jax.random.permutation(jax.random.fold_in(own, 1), rows)]
    rotation = jax.random.randint(jax.random.fold_in(own, 2), (rows, 1), 0, top)
    return jnp.take_along_axis(grid, (jnp.arange(top)[None, :] + rotation) % top, axis=1)


def portions_of(count, total, limit, skew, full):
    loads = [(1 << 20) // math.isqrt(rank ** skew) + 1 for rank in range(1, count + 1)]
    largest = limit if full else min(limit, max(-(-total // count), total * loads[0] // sum(loads)))
    least = 1 if total - largest >= count - 1 else 0
    counts, rest = [largest] + [least] * (count - 1), total - largest - least * (count - 1)
    while rest > 0:
        free = [i for i in range(1, count) if counts[i] < largest] or [i for i in range(1, count) if counts[i] < limit]
        whole, remaining = sum([loads[i] for i in free]), rest
        for i in free:
            more = min(limit - counts[i], max(1, remaining * loads[i] // whole), rest)
            counts[i] = counts[i] + more
            rest = rest - more
    return np.array(counts)


def bell_draw(own_key, shape, width, bound, pieces=(), kind=jnp.bfloat16):
    array = width * jax.random.normal(own_key, shape, jnp.float32)
    if pieces:
        array = array * levels(own_key, shape, pieces, -0.22, 0.18)
    return jnp.clip(array, -bound, bound).astype(kind)


def setup_inputs(seed: int = 0) -> dict:
    streams_of = jax.random.split(jax.random.key(seed), 7)
    adjoint = bell_draw(streams_of[0], (F, NX, NR, NA), 1.0, 6.0, ((1, 32), (2, 2), (3, 8)), jnp.float32)
    coeff = jnp.clip(0.5 + 1.5 * jax.random.uniform(streams_of[1], (3, NX, NR, NA), jnp.float32) ** levels(streams_of[1], (3, NX, NR, NA), ((1, 32), (2, 2), (3, 8)), -0.2, 0.2), 0.5, 2.0)
    flux = bell_draw(streams_of[2], (3, F, F), (3 * F) ** -0.5, 1.5, (), jnp.float32)
    target_cell = touch_ends(jax.random.randint(streams_of[3], (TARGETS,), 0, CX * CR * CA), jax.random.fold_in(streams_of[3], 1), 0, (CX * CR * CA) - 1).astype(jnp.int32)
    donor_owner_keys = jax.random.split(jax.random.fold_in(streams_of[4], 1), TARGETS // TGT)
    donor_owner_turns = jax.random.permutation(jax.random.fold_in(streams_of[4], 3), TARGETS // TGT)
    donor_owner = jax.vmap(lambda own, number: assign_block(jax.random.fold_in(streams_of[4], 2), own, number, TGT, N_GX, 1, CAP, 2))(donor_owner_keys, donor_owner_turns).reshape((TARGETS, 1))
    donor_cell = touch_ends(jax.random.randint(streams_of[5], (TARGETS,), 0, CX * CR * CA), jax.random.fold_in(streams_of[5], 1), 0, (CX * CR * CA) - 1).astype(jnp.int32)
    return dict(adjoint=adjoint, coeff=coeff, flux=flux, target_cell=target_cell, donor_owner=donor_owner, donor_cell=donor_cell)


filter_alpha = 0.49
sat_gain = 0.5
pade_coeffs = [(193.0 + 126.0 * filter_alpha) / 256.0, (105.0 + 302.0 * filter_alpha) / 256.0, 15.0 * (2.0 * filter_alpha - 1.0) / 64.0, 45.0 * (1.0 - 2.0 * filter_alpha) / 512.0, 5.0 * (2.0 * filter_alpha - 1.0) / 256.0, (1.0 - 2.0 * filter_alpha) / 512.0]


def reference(adjoint, coeff, flux, target_cell, donor_owner, donor_cell):
    wave = jnp.arange(NA // 2 + 1).astype(jnp.float32) * (2.0 * math.pi / NA)
    numer = jnp.full(wave.shape, pade_coeffs[0], jnp.float32)
    for order in range(1, 6):
        numer = numer + pade_coeffs[order] * jnp.cos(order * wave)
    denom = 1.0 + 2.0 * filter_alpha * jnp.cos(wave)
    spectrum = jnp.fft.rfft(adjoint, axis=3) * (numer / denom)
    filtered = jnp.fft.irfft(spectrum, n=NA, axis=3).astype(jnp.float32)
    padded = jnp.pad(filtered, ((0, 0), (1, 1), (1, 1), (0, 0)))
    along_x = padded[:, 2:, 1:-1, :] - padded[:, :-2, 1:-1, :]
    along_r = padded[:, 1:-1, 2:, :] - padded[:, 1:-1, :-2, :]
    along_a = jnp.roll(filtered, -1, axis=3) - jnp.roll(filtered, 1, axis=3)
    gradient = filtered
    for direction, change in enumerate((along_x, along_r, along_a)):
        mixing = jnp.einsum("fg,fxra->gxra", flux[direction], change, precision=lax.Precision.HIGHEST)
        gradient = gradient + coeff[direction][None] * mixing
    device = jnp.arange(TARGETS, dtype=jnp.int32) // TGT
    slab_index = device // (N_AZ * N_ROW)
    sector = (device // N_ROW) % N_AZ
    radial_band = device % N_ROW

    def global_index(streams, cell):
        cell_x = cell // (CR * CA)
        cell_r = (cell // CA) % CR
        cell_a = cell % CA
        return ((streams * CX + cell_x) * NR + radial_band * CR + cell_r) * NA + sector * CA + cell_a

    target_flat = global_index(slab_index, target_cell)
    donor_flat = global_index(donor_owner[:, 0], donor_cell)
    source = sat_gain * filtered.reshape(F, -1)[:, target_flat]
    flat_grad = gradient.reshape(F, -1)
    flat_grad = flat_grad.at[:, donor_flat].add(source)
    flat_grad = flat_grad.at[:, target_flat].add(-source)
    return flat_grad.reshape(adjoint.shape)
```

```python
import jax
import jax.numpy as jnp
import numpy as np
from jax import lax
from jax.sharding import PartitionSpec as P

filter_alpha = 0.49
sat_gain = 0.5
pade_coeffs = [
    (193.0 + 126.0 * filter_alpha) / 256.0,
    (105.0 + 302.0 * filter_alpha) / 256.0,
    15.0 * (2.0 * filter_alpha - 1.0) / 64.0,
    45.0 * (1.0 - 2.0 * filter_alpha) / 512.0,
    5.0 * (2.0 * filter_alpha - 1.0) / 256.0,
    (1.0 - 2.0 * filter_alpha) / 512.0,
]
HI = lax.Precision.HIGHEST


def loop_weights(length):
    wave = np.arange(length // 2 + 1) * (2.0 * np.pi / length)
    numer = np.full(wave.shape, pade_coeffs[0])
    for order in range(1, 6):
        numer = numer + pade_coeffs[order] * np.cos(order * wave)
    denom = 1.0 + 2.0 * filter_alpha * np.cos(wave)
    return np.fft.irfft(numer / denom, n=length)


def block_tables(cells, length):
    w = loop_weights(length)
    c = np.arange(cells)[:, None]
    o = np.arange(cells)[None, :]
    tables = []
    for shift in (-1, 0, 1):
        base = o - c - shift * cells
        filt = w[base % length]
        diff = w[(base + 1) % length] - w[(base - 1) % length]
        tables.append(np.concatenate([filt, diff], axis=1).astype(np.float32))
    return tables


def neighbours(value, axis, wrap):
    size = lax.axis_size(axis)
    up = [(i, (i + 1) % size) for i in range(size if wrap else size - 1)]
    down = [(j, i) for i, j in up]
    return up, down


def shards(adjoint, coeff, flux, target_cell, donor_owner, donor_cell):
    fields, rows_x, rows_r, cells_a = adjoint.shape
    loop_span = cells_a * lax.axis_size("az")
    rows = rows_x * rows_r
    tables = block_tables(cells_a, loop_span)

    up, down = neighbours(adjoint, "az", True)
    left = lax.ppermute(adjoint, "az", up)
    right = lax.ppermute(adjoint, "az", down)
    both = jnp.zeros((fields, rows_x, rows_r, 2 * cells_a), jnp.float32)
    for block, table in zip((left, adjoint, right), tables):
        both = both + jnp.einsum("fxra,ao->fxro", block, jnp.asarray(table), precision=HI)
    filtered = both[..., :cells_a]
    along_a = both[..., cells_a:]

    up_x, down_x = neighbours(filtered, "gx", False)
    before_x = lax.ppermute(filtered[:, -1:], "gx", up_x)
    after_x = lax.ppermute(filtered[:, :1], "gx", down_x)
    up_r, down_r = neighbours(filtered, "row", False)
    before_r = lax.ppermute(filtered[:, :, -1:], "row", up_r)
    after_r = lax.ppermute(filtered[:, :, :1], "row", down_r)
    along_x = jnp.concatenate([filtered[:, 1:], after_x], axis=1) - jnp.concatenate(
        [before_x, filtered[:, :-1]], axis=1
    )
    along_r = jnp.concatenate([filtered[:, :, 1:], after_r], axis=2) - jnp.concatenate(
        [before_r, filtered[:, :, :-1]], axis=2
    )
    gradient = filtered
    for direction, change in enumerate((along_x, along_r, along_a)):
        mixing = jnp.einsum("fg,fxra->gxra", flux[direction], change, precision=HI)
        gradient = gradient + coeff[direction][None] * mixing

    row_ids = jnp.arange(rows, dtype=jnp.int32)
    lane_ids = jnp.arange(cells_a, dtype=jnp.int32)
    t_rows = (target_cell[:, None] // cells_a == row_ids[None, :]).astype(jnp.float32)
    t_lanes = (target_cell[:, None] % cells_a == lane_ids[None, :]).astype(jnp.float32)
    flat = filtered.reshape(fields, rows, cells_a)
    picked = jnp.einsum("tk,fka->fta", t_rows, flat, precision=HI)
    source = sat_gain * jnp.sum(picked * t_lanes[None], axis=2)

    owner_rows = donor_owner[:, 0]
    owners = lax.axis_size("gx")
    capacity = target_cell.shape[0] // 8
    onehot = (owner_rows[:, None] == jnp.arange(owners, dtype=jnp.int32)[None, :]).astype(jnp.int32)
    slot_rank = jnp.sum(onehot * (jnp.cumsum(onehot, axis=0) - 1), axis=1)
    slot_place = owner_rows * capacity + slot_rank
    packed = jnp.concatenate([source, donor_cell.astype(jnp.float32)[None, :]], axis=0)
    slots = (slot_place[:, None] == jnp.arange(owners * capacity, dtype=jnp.int32)[None, :]).astype(
        jnp.float32
    )
    outbox = jnp.einsum("pt,ts->ps", packed, slots, precision=HI)
    received = lax.all_to_all(
        outbox.reshape(fields + 1, owners, capacity), "gx", split_axis=1, concat_axis=1, tiled=True
    )
    received = received.reshape(fields + 1, owners * capacity)
    got_cell = received[fields].astype(jnp.int32)
    d_rows = (got_cell[:, None] // cells_a == row_ids[None, :]).astype(jnp.float32)
    d_lanes = (got_cell[:, None] % cells_a == lane_ids[None, :]).astype(jnp.float32)

    all_rows = jnp.concatenate([t_rows, d_rows], axis=0)
    all_lanes = jnp.concatenate([t_lanes, d_lanes], axis=0)
    amounts = jnp.concatenate([-source, received[:fields]], axis=1)
    spread = amounts[:, :, None] * all_lanes[None]
    update = jnp.einsum("nk,fna->fka", all_rows, spread, precision=HI)
    return gradient + update.reshape(adjoint.shape)


def solution(mesh):
    return jax.shard_map(
        shards,
        mesh=mesh,
        in_specs=(
            P(None, "gx", "row", "az"),
            P(None, "gx", "row", "az"),
            P(),
            P(("gx", "az", "row")),
            P(("gx", "az", "row"), None),
            P(("gx", "az", "row")),
        ),
        out_specs=P(None, "gx", "row", "az"),
        check_vma=False,
    )
```

```python
import jax
import jax.numpy as jnp
import numpy as np
from jax import lax
from jax.sharding import PartitionSpec as P

filter_alpha = 0.49
sat_gain = 0.5
pade_coeffs = [
    (193.0 + 126.0 * filter_alpha) / 256.0,
    (105.0 + 302.0 * filter_alpha) / 256.0,
    15.0 * (2.0 * filter_alpha - 1.0) / 64.0,
    45.0 * (1.0 - 2.0 * filter_alpha) / 512.0,
    5.0 * (2.0 * filter_alpha - 1.0) / 256.0,
    (1.0 - 2.0 * filter_alpha) / 512.0,
]
HI = lax.Precision.HIGHEST


root_value = (-1.0 + (1.0 - 4.0 * filter_alpha * filter_alpha) ** 0.5) / (2.0 * filter_alpha)
green_scale = 1.0 / (1.0 + 2.0 * filter_alpha * root_value)
EDGE = 7


def stencil_weight(shift):
    return pade_coeffs[0] if shift == 0 else 0.5 * pade_coeffs[abs(shift)]


def loop_weight(offset, length):
    total = np.zeros(np.shape(offset))
    for shift in range(-5, 6):
        n = np.mod(offset - shift, length)
        images = root_value ** n + root_value ** (length - n)
        total = total + stencil_weight(shift) * green_scale * images / (1.0 - root_value**length)
    return total


def halo_tables(cells, length):
    r = root_value
    tail = green_scale / (1.0 - r**length) * sum(stencil_weight(s) * r ** (-s) for s in range(-5, 6))
    c = np.arange(cells)[:, None]
    o = np.arange(cells)[None, :]

    def both(distance):
        return np.concatenate(
            [loop_weight(distance, length), loop_weight(distance + 1, length) - loop_weight(distance - 1, length)],
            axis=-1,
        )

    own = both(o - c)
    k = np.arange(EDGE)[:, None]
    ov = np.arange(cells)[None, :]
    send_right = np.zeros((cells, EDGE + 1))
    send_right[cells - EDGE + np.arange(EDGE), np.arange(EDGE)] = 1.0
    send_right[: cells - EDGE, EDGE] = r ** (cells - np.arange(cells - EDGE))
    from_left = np.concatenate(
        [both(ov + cells - (cells - EDGE + k)),
         np.concatenate([tail * r**ov, tail * r**ov * (r - 1.0 / r)], axis=-1)],
        axis=0,
    )
    send_left = np.zeros((cells, EDGE + 1))
    send_left[np.arange(EDGE), np.arange(EDGE)] = 1.0
    send_left[EDGE:, EDGE] = r ** (np.arange(EDGE, cells) + 1.0)
    from_right = np.concatenate(
        [both(ov - cells - k),
         np.concatenate([tail * r ** (cells - 1 - ov), tail * r ** (cells - 1 - ov) * (1.0 / r - r)], axis=-1)],
        axis=0,
    )
    return [np.asarray(t, np.float32) for t in (own, send_right, from_left, send_left, from_right)]


def neighbours(value, axis, wrap):
    size = lax.axis_size(axis)
    up = [(i, (i + 1) % size) for i in range(size if wrap else size - 1)]
    down = [(j, i) for i, j in up]
    return up, down


def shards(adjoint, coeff, flux, target_cell, donor_owner, donor_cell):
    fields, rows_x, rows_r, cells_a = adjoint.shape
    loop_span = cells_a * lax.axis_size("az")
    rows = rows_x * rows_r
    own_t, send_right_t, from_left_t, send_left_t, from_right_t = halo_tables(cells_a, loop_span)
    lines = adjoint.reshape(fields * rows, cells_a)

    up, down = neighbours(adjoint, "az", True)
    to_right = jnp.einsum("lc,ck->kl", lines, jnp.asarray(send_right_t), precision=HI)
    to_left = jnp.einsum("lc,ck->kl", lines, jnp.asarray(send_left_t), precision=HI)
    from_left = lax.ppermute(to_right, "az", up)
    from_right = lax.ppermute(to_left, "az", down)
    both = jnp.einsum("lc,co->lo", lines, jnp.asarray(own_t), precision=HI)
    both = both + jnp.einsum("kl,ko->lo", from_left, jnp.asarray(from_left_t), precision=HI)
    both = both + jnp.einsum("kl,ko->lo", from_right, jnp.asarray(from_right_t), precision=HI)
    both = both.reshape(fields, rows_x, rows_r, 2 * cells_a)
    filtered = both[..., :cells_a]
    along_a = both[..., cells_a:]

    up_x, down_x = neighbours(filtered, "gx", False)
    before_x = lax.ppermute(filtered[:, -1:], "gx", up_x)
    after_x = lax.ppermute(filtered[:, :1], "gx", down_x)
    up_r, down_r = neighbours(filtered, "row", False)
    before_r = lax.ppermute(filtered[:, :, -1:], "row", up_r)
    after_r = lax.ppermute(filtered[:, :, :1], "row", down_r)
    along_x = jnp.concatenate([filtered[:, 1:], after_x], axis=1) - jnp.concatenate(
        [before_x, filtered[:, :-1]], axis=1
    )
    along_r = jnp.concatenate([filtered[:, :, 1:], after_r], axis=2) - jnp.concatenate(
        [before_r, filtered[:, :, :-1]], axis=2
    )
    gradient = filtered
    for direction, change in enumerate((along_x, along_r, along_a)):
        mixing = jnp.einsum("fg,fxra->gxra", flux[direction], change, precision=HI)
        gradient = gradient + coeff[direction][None] * mixing

    row_ids = jnp.arange(rows, dtype=jnp.int32)
    lane_ids = jnp.arange(cells_a, dtype=jnp.int32)
    t_rows = (target_cell[:, None] // cells_a == row_ids[None, :]).astype(jnp.float32)
    t_lanes = (target_cell[:, None] % cells_a == lane_ids[None, :]).astype(jnp.float32)
    flat = filtered.reshape(fields, rows, cells_a)
    picked = jnp.einsum("tk,fka->fta", t_rows, flat, precision=HI)
    source = sat_gain * jnp.sum(picked * t_lanes[None], axis=2)

    owner_rows = donor_owner[:, 0]
    owners = lax.axis_size("gx")
    capacity = target_cell.shape[0] // 8
    onehot = (owner_rows[:, None] == jnp.arange(owners, dtype=jnp.int32)[None, :]).astype(jnp.int32)
    slot_rank = jnp.sum(onehot * (jnp.cumsum(onehot, axis=0) - 1), axis=1)
    slot_place = owner_rows * capacity + slot_rank
    packed = jnp.concatenate([source, donor_cell.astype(jnp.float32)[None, :]], axis=0)
    slots = (slot_place[:, None] == jnp.arange(owners * capacity, dtype=jnp.int32)[None, :]).astype(
        jnp.float32
    )
    outbox = jnp.einsum("pt,ts->ps", packed, slots, precision=HI)
    received = lax.all_to_all(
        outbox.reshape(fields + 1, owners, capacity), "gx", split_axis=1, concat_axis=1, tiled=True
    )
    received = received.reshape(fields + 1, owners * capacity)
    got_cell = received[fields].astype(jnp.int32)
    d_rows = (got_cell[:, None] // cells_a == row_ids[None, :]).astype(jnp.float32)
    d_lanes = (got_cell[:, None] % cells_a == lane_ids[None, :]).astype(jnp.float32)

    all_rows = jnp.concatenate([t_rows, d_rows], axis=0)
    all_lanes = jnp.concatenate([t_lanes, d_lanes], axis=0)
    amounts = jnp.concatenate([-source, received[:fields]], axis=1)
    spread = amounts[:, :, None] * all_lanes[None]
    update = jnp.einsum("nk,fna->fka", all_rows, spread, precision=HI)
    return gradient + update.reshape(adjoint.shape)


def solution(mesh):
    return jax.shard_map(
        shards,
        mesh=mesh,
        in_specs=(
            P(None, "gx", "row", "az"),
            P(None, "gx", "row", "az"),
            P(),
            P(("gx", "az", "row")),
            P(("gx", "az", "row"), None),
            P(("gx", "az", "row")),
        ),
        out_specs=P(None, "gx", "row", "az"),
        check_vma=False,
    )
```

```python
import jax
import jax.numpy as jnp
import numpy as np
from jax import lax
from jax.sharding import PartitionSpec as P

filter_alpha = 0.49
sat_gain = 0.5
pade_coeffs = [
    (193.0 + 126.0 * filter_alpha) / 256.0,
    (105.0 + 302.0 * filter_alpha) / 256.0,
    15.0 * (2.0 * filter_alpha - 1.0) / 64.0,
    45.0 * (1.0 - 2.0 * filter_alpha) / 512.0,
    5.0 * (2.0 * filter_alpha - 1.0) / 256.0,
    (1.0 - 2.0 * filter_alpha) / 512.0,
]
HI = lax.Precision.HIGHEST


root_value = (-1.0 + (1.0 - 4.0 * filter_alpha * filter_alpha) ** 0.5) / (2.0 * filter_alpha)
green_scale = 1.0 / (1.0 + 2.0 * filter_alpha * root_value)
EDGE = 7


def stencil_weight(shift):
    return pade_coeffs[0] if shift == 0 else 0.5 * pade_coeffs[abs(shift)]


def loop_weight(offset, length):
    total = np.zeros(np.shape(offset))
    for shift in range(-5, 6):
        n = np.mod(offset - shift, length)
        images = root_value ** n + root_value ** (length - n)
        total = total + stencil_weight(shift) * green_scale * images / (1.0 - root_value**length)
    return total


def halo_tables(cells, length):
    r = root_value
    tail = green_scale / (1.0 - r**length) * sum(stencil_weight(s) * r ** (-s) for s in range(-5, 6))
    c = np.arange(cells)[:, None]
    o = np.arange(cells)[None, :]

    def both(distance):
        return np.concatenate(
            [loop_weight(distance, length), loop_weight(distance + 1, length) - loop_weight(distance - 1, length)],
            axis=-1,
        )

    own = both(o - c)
    k = np.arange(EDGE)[:, None]
    ov = np.arange(cells)[None, :]
    send_right = np.zeros((cells, EDGE + 1))
    send_right[cells - EDGE + np.arange(EDGE), np.arange(EDGE)] = 1.0
    send_right[: cells - EDGE, EDGE] = r ** (cells - np.arange(cells - EDGE))
    from_left = np.concatenate(
        [both(ov + cells - (cells - EDGE + k)),
         np.concatenate([tail * r**ov, tail * r**ov * (r - 1.0 / r)], axis=-1)],
        axis=0,
    )
    send_left = np.zeros((cells, EDGE + 1))
    send_left[np.arange(EDGE), np.arange(EDGE)] = 1.0
    send_left[EDGE:, EDGE] = r ** (np.arange(EDGE, cells) + 1.0)
    from_right = np.concatenate(
        [both(ov - cells - k),
         np.concatenate([tail * r ** (cells - 1 - ov), tail * r ** (cells - 1 - ov) * (1.0 / r - r)], axis=-1)],
        axis=0,
    )
    return [np.asarray(t, np.float32) for t in (own, send_right, from_left, send_left, from_right)]


def neighbours(value, axis, wrap):
    size = lax.axis_size(axis)
    up = [(i, (i + 1) % size) for i in range(size if wrap else size - 1)]
    down = [(j, i) for i, j in up]
    return up, down


def shards(adjoint, coeff, flux, target_cell, donor_owner, donor_cell):
    fields, rows_x, rows_r, cells_a = adjoint.shape
    loop_span = cells_a * lax.axis_size("az")
    rows = rows_x * rows_r
    own_t, send_right_t, from_left_t, send_left_t, from_right_t = halo_tables(cells_a, loop_span)
    lines = adjoint.reshape(fields * rows, cells_a)

    up, down = neighbours(adjoint, "az", True)
    to_right = jnp.einsum("lc,ck->kl", lines, jnp.asarray(send_right_t), precision=HI)
    to_left = jnp.einsum("lc,ck->kl", lines, jnp.asarray(send_left_t), precision=HI)
    from_left = lax.ppermute(to_right, "az", up)
    from_right = lax.ppermute(to_left, "az", down)
    both = jnp.einsum("lc,co->lo", lines, jnp.asarray(own_t), precision=HI)
    both = both + jnp.einsum("kl,ko->lo", from_left, jnp.asarray(from_left_t), precision=HI)
    both = both + jnp.einsum("kl,ko->lo", from_right, jnp.asarray(from_right_t), precision=HI)
    both = both.reshape(fields, rows_x, rows_r, 2 * cells_a)
    filtered = both[..., :cells_a]
    along_a = both[..., cells_a:]

    up_x, down_x = neighbours(filtered, "gx", False)
    before_x = lax.ppermute(filtered[:, -1:], "gx", up_x)
    after_x = lax.ppermute(filtered[:, :1], "gx", down_x)
    up_r, down_r = neighbours(filtered, "row", False)
    before_r = lax.ppermute(filtered[:, :, -1:], "row", up_r)
    after_r = lax.ppermute(filtered[:, :, :1], "row", down_r)
    along_x = jnp.concatenate([filtered[:, 1:], after_x], axis=1) - jnp.concatenate(
        [before_x, filtered[:, :-1]], axis=1
    )
    along_r = jnp.concatenate([filtered[:, :, 1:], after_r], axis=2) - jnp.concatenate(
        [before_r, filtered[:, :, :-1]], axis=2
    )
    gradient = filtered
    for direction, change in enumerate((along_x, along_r, along_a)):
        mixing = jnp.einsum("fg,fxra->gxra", flux[direction], change, precision=HI)
        gradient = gradient + coeff[direction][None] * mixing

    row_ids = jnp.arange(rows, dtype=jnp.int32)
    lane_ids = jnp.arange(cells_a, dtype=jnp.int32)
    t_rows = (target_cell[:, None] // cells_a == row_ids[None, :]).astype(jnp.float32)
    t_lanes = (target_cell[:, None] % cells_a == lane_ids[None, :]).astype(jnp.float32)
    flat = filtered.reshape(fields, rows, cells_a)
    picked = jnp.einsum("tk,fka->fta", t_rows, flat, precision=HI)
    source = sat_gain * jnp.sum(picked * t_lanes[None], axis=2)

    owner_rows = donor_owner[:, 0]
    owners = lax.axis_size("gx")
    capacity = target_cell.shape[0] // 8
    onehot = (owner_rows[:, None] == jnp.arange(owners, dtype=jnp.int32)[None, :]).astype(jnp.int32)
    slot_rank = jnp.sum(onehot * (jnp.cumsum(onehot, axis=0) - 1), axis=1)
    slot_place = owner_rows * capacity + slot_rank
    code = (slot_place).astype(jnp.float32)
    pad = jnp.zeros((1, source.shape[1]), jnp.float32)
    packed = jnp.concatenate([source, donor_cell.astype(jnp.float32)[None, :], code[None, :], pad], axis=0)
    gathered = lax.all_gather(packed, "gx", axis=0)
    first_slot = lax.axis_index("gx") * capacity
    keep = (
        gathered[:, fields + 1, :, None].astype(jnp.int32)
        == first_slot + jnp.arange(capacity, dtype=jnp.int32)[None, None, :]
    ).astype(jnp.float32)
    compact = jnp.einsum("spt,stk->psk", gathered[:, : fields + 1], keep, precision=HI)
    received = compact.reshape(fields + 1, owners * capacity)
    got_cell = received[fields].astype(jnp.int32)
    d_rows = (got_cell[:, None] // cells_a == row_ids[None, :]).astype(jnp.float32)
    d_lanes = (got_cell[:, None] % cells_a == lane_ids[None, :]).astype(jnp.float32)

    all_rows = jnp.concatenate([t_rows, d_rows], axis=0)
    all_lanes = jnp.concatenate([t_lanes, d_lanes], axis=0)
    amounts = jnp.concatenate([-source, received[:fields]], axis=1)
    spread = amounts[:, :, None] * all_lanes[None]
    update = jnp.einsum("nk,fna->fka", all_rows, spread, precision=HI)
    return gradient + update.reshape(adjoint.shape)


def solution(mesh):
    return jax.shard_map(
        shards,
        mesh=mesh,
        in_specs=(
            P(None, "gx", "row", "az"),
            P(None, "gx", "row", "az"),
            P(),
            P(("gx", "az", "row")),
            P(("gx", "az", "row"), None),
            P(("gx", "az", "row")),
        ),
        out_specs=P(None, "gx", "row", "az"),
        check_vma=False,
    )
```

```python
import jax
import jax.numpy as jnp
import numpy as np
from jax import lax
from jax.sharding import PartitionSpec as P

filter_alpha = 0.49
sat_gain = 0.5
pade_coeffs = [
    (193.0 + 126.0 * filter_alpha) / 256.0,
    (105.0 + 302.0 * filter_alpha) / 256.0,
    15.0 * (2.0 * filter_alpha - 1.0) / 64.0,
    45.0 * (1.0 - 2.0 * filter_alpha) / 512.0,
    5.0 * (2.0 * filter_alpha - 1.0) / 256.0,
    (1.0 - 2.0 * filter_alpha) / 512.0,
]
HI = lax.Precision.HIGHEST


root_value = (-1.0 + (1.0 - 4.0 * filter_alpha * filter_alpha) ** 0.5) / (2.0 * filter_alpha)
green_scale = 1.0 / (1.0 + 2.0 * filter_alpha * root_value)
EDGE = 7


def stencil_weight(shift):
    return pade_coeffs[0] if shift == 0 else 0.5 * pade_coeffs[abs(shift)]


def loop_weight(offset, length):
    total = np.zeros(np.shape(offset))
    for shift in range(-5, 6):
        n = np.mod(offset - shift, length)
        images = root_value ** n + root_value ** (length - n)
        total = total + stencil_weight(shift) * green_scale * images / (1.0 - root_value**length)
    return total


def halo_tables(cells, length):
    r = root_value
    tail = green_scale / (1.0 - r**length) * sum(stencil_weight(s) * r ** (-s) for s in range(-5, 6))
    c = np.arange(cells)[:, None]
    o = np.arange(cells)[None, :]

    def both(distance):
        return np.concatenate(
            [loop_weight(distance, length), loop_weight(distance + 1, length) - loop_weight(distance - 1, length)],
            axis=-1,
        )

    own = both(o - c)
    k = np.arange(EDGE)[:, None]
    ov = np.arange(cells)[None, :]
    send_right = np.zeros((cells, EDGE + 1))
    send_right[cells - EDGE + np.arange(EDGE), np.arange(EDGE)] = 1.0
    send_right[: cells - EDGE, EDGE] = r ** (cells - np.arange(cells - EDGE))
    from_left = np.concatenate(
        [both(ov + cells - (cells - EDGE + k)),
         np.concatenate([tail * r**ov, tail * r**ov * (r - 1.0 / r)], axis=-1)],
        axis=0,
    )
    send_left = np.zeros((cells, EDGE + 1))
    send_left[np.arange(EDGE), np.arange(EDGE)] = 1.0
    send_left[EDGE:, EDGE] = r ** (np.arange(EDGE, cells) + 1.0)
    from_right = np.concatenate(
        [both(ov - cells - k),
         np.concatenate([tail * r ** (cells - 1 - ov), tail * r ** (cells - 1 - ov) * (1.0 / r - r)], axis=-1)],
        axis=0,
    )
    return [np.asarray(t, np.float32) for t in (own, send_right, from_left, send_left, from_right)]


def neighbours(value, axis, wrap):
    size = lax.axis_size(axis)
    up = [(i, (i + 1) % size) for i in range(size if wrap else size - 1)]
    down = [(j, i) for i, j in up]
    return up, down


def shards(adjoint, coeff, flux, target_cell, donor_owner, donor_cell):
    fields, rows_x, rows_r, cells_a = adjoint.shape
    loop_span = cells_a * lax.axis_size("az")
    rows = rows_x * rows_r
    own_t, send_right_t, from_left_t, send_left_t, from_right_t = halo_tables(cells_a, loop_span)
    lines = adjoint.reshape(fields * rows, cells_a)

    up, down = neighbours(adjoint, "az", True)
    right_moment = jnp.asarray(send_right_t[:, EDGE])
    left_moment = jnp.asarray(send_left_t[:, EDGE])
    to_right = jnp.concatenate(
        [lines[:, cells_a - EDGE :], jnp.sum(lines * right_moment[None], axis=1, keepdims=True)], axis=1
    ).T
    to_left = jnp.concatenate(
        [lines[:, :EDGE], jnp.sum(lines * left_moment[None], axis=1, keepdims=True)], axis=1
    ).T
    from_left = lax.ppermute(to_right, "az", up)
    from_right = lax.ppermute(to_left, "az", down)
    both = jnp.einsum("lc,co->lo", lines, jnp.asarray(own_t), precision=HI)
    both = both + jnp.einsum("kl,ko->lo", from_left, jnp.asarray(from_left_t), precision=HI)
    both = both + jnp.einsum("kl,ko->lo", from_right, jnp.asarray(from_right_t), precision=HI)
    both = both.reshape(fields, rows_x, rows_r, 2 * cells_a)
    filtered = both[..., :cells_a]
    along_a = both[..., cells_a:]

    row_ids = jnp.arange(rows, dtype=jnp.int32)
    lane_ids = jnp.arange(cells_a, dtype=jnp.int32)
    t_rows = (target_cell[:, None] // cells_a == row_ids[None, :]).astype(jnp.float32)
    t_lanes = (target_cell[:, None] % cells_a == lane_ids[None, :]).astype(jnp.float32)
    flat = filtered.reshape(fields, rows, cells_a)
    picked = jnp.einsum("tk,fka->fta", t_rows, flat, precision=HI)
    source = sat_gain * jnp.sum(picked * t_lanes[None], axis=2)

    owner_rows = donor_owner[:, 0]
    owners = lax.axis_size("gx")
    capacity = target_cell.shape[0] // 8
    onehot = (owner_rows[:, None] == jnp.arange(owners, dtype=jnp.int32)[None, :]).astype(jnp.int32)
    slot_rank = jnp.sum(onehot * (jnp.cumsum(onehot, axis=0) - 1), axis=1)
    slot_place = owner_rows * capacity + slot_rank
    packed = jnp.concatenate([source, donor_cell.astype(jnp.float32)[None, :]], axis=0)
    slots = (
        slot_place[:, None, None]
        == (jnp.arange(owners, dtype=jnp.int32)[:, None] * capacity + jnp.arange(capacity, dtype=jnp.int32))[None]
    ).astype(jnp.float32)
    outbox = jnp.einsum("pt,tos->ops", packed, slots, precision=HI).reshape(owners, (fields + 1) * capacity)
    received = lax.all_to_all(outbox, "gx", split_axis=0, concat_axis=0, tiled=True)
    taken = jnp.einsum("nk,fna->fka", t_rows, -source[:, :, None] * t_lanes[None], precision=HI)
    up_x, down_x = neighbours(filtered, "gx", False)
    last_x, first_x, last_r, first_r = filtered[:, -1], filtered[:, 0], filtered[:, :, -1], filtered[:, :, 0]
    before_x = lax.ppermute(last_x, "gx", up_x)[:, None]
    after_x = lax.ppermute(first_x, "gx", down_x)[:, None]
    if lax.axis_size("row") == 2:
        band = lax.axis_index("row")
        other = lax.ppermute(jnp.where(band == 0, last_r, first_r), "row", [(0, 1), (1, 0)])
        before_r = jnp.where(band == 1, other, 0.0)[:, :, None]
        after_r = jnp.where(band == 0, other, 0.0)[:, :, None]
    else:
        up_r, down_r = neighbours(filtered, "row", False)
        before_r = lax.ppermute(last_r, "row", up_r)[:, :, None]
        after_r = lax.ppermute(first_r, "row", down_r)[:, :, None]
    along_x = jnp.concatenate([filtered[:, 1:], after_x], axis=1) - jnp.concatenate(
        [before_x, filtered[:, :-1]], axis=1
    )
    along_r = jnp.concatenate([filtered[:, :, 1:], after_r], axis=2) - jnp.concatenate(
        [before_r, filtered[:, :, :-1]], axis=2
    )
    gradient = filtered
    for direction, change in enumerate((along_x, along_r, along_a)):
        mixing = jnp.einsum("fg,fxra->gxra", flux[direction], change, precision=HI)
        gradient = gradient + coeff[direction][None] * mixing
    gradient = gradient + taken.reshape(adjoint.shape)

    received = received.reshape(owners, fields + 1, capacity).transpose(1, 0, 2).reshape(fields + 1, owners * capacity)
    got_cell = received[fields].astype(jnp.int32)
    d_rows = (got_cell[:, None] // cells_a == row_ids[None, :]).astype(jnp.float32)
    d_lanes = (got_cell[:, None] % cells_a == lane_ids[None, :]).astype(jnp.float32)
    spread = received[:fields, :, None] * d_lanes[None]
    update = jnp.einsum("nk,fna->fka", d_rows, spread, precision=HI)
    return gradient + update.reshape(adjoint.shape)


def solution(mesh):
    return jax.shard_map(
        shards,
        mesh=mesh,
        in_specs=(
            P(None, "gx", "row", "az"),
            P(None, "gx", "row", "az"),
            P(),
            P(("gx", "az", "row")),
            P(("gx", "az", "row"), None),
            P(("gx", "az", "row")),
        ),
        out_specs=P(None, "gx", "row", "az"),
        check_vma=False,
    )
```

```python
import jax
import jax.numpy as jnp
import numpy as np
from jax import lax
from jax.sharding import PartitionSpec as P

filter_alpha = 0.49
sat_gain = 0.5
pade_coeffs = [
    (193.0 + 126.0 * filter_alpha) / 256.0,
    (105.0 + 302.0 * filter_alpha) / 256.0,
    15.0 * (2.0 * filter_alpha - 1.0) / 64.0,
    45.0 * (1.0 - 2.0 * filter_alpha) / 512.0,
    5.0 * (2.0 * filter_alpha - 1.0) / 256.0,
    (1.0 - 2.0 * filter_alpha) / 512.0,
]
HI = lax.Precision.HIGHEST


root_value = (-1.0 + (1.0 - 4.0 * filter_alpha * filter_alpha) ** 0.5) / (2.0 * filter_alpha)
green_scale = 1.0 / (1.0 + 2.0 * filter_alpha * root_value)
EDGE = 7


def stencil_weight(shift):
    return pade_coeffs[0] if shift == 0 else 0.5 * pade_coeffs[abs(shift)]


def loop_weight(offset, length):
    total = np.zeros(np.shape(offset))
    for shift in range(-5, 6):
        n = np.mod(offset - shift, length)
        images = root_value ** n + root_value ** (length - n)
        total = total + stencil_weight(shift) * green_scale * images / (1.0 - root_value**length)
    return total


def halo_tables(cells, length):
    r = root_value
    tail = green_scale / (1.0 - r**length) * sum(stencil_weight(s) * r ** (-s) for s in range(-5, 6))
    c = np.arange(cells)[:, None]
    o = np.arange(cells)[None, :]

    def both(distance):
        return np.concatenate(
            [loop_weight(distance, length), loop_weight(distance + 1, length) - loop_weight(distance - 1, length)],
            axis=-1,
        )

    own = both(o - c)
    k = np.arange(EDGE)[:, None]
    ov = np.arange(cells)[None, :]
    send_right = np.zeros((cells, EDGE + 1))
    send_right[cells - EDGE + np.arange(EDGE), np.arange(EDGE)] = 1.0
    send_right[: cells - EDGE, EDGE] = r ** (cells - np.arange(cells - EDGE))
    from_left = np.concatenate(
        [both(ov + cells - (cells - EDGE + k)),
         np.concatenate([tail * r**ov, tail * r**ov * (r - 1.0 / r)], axis=-1)],
        axis=0,
    )
    send_left = np.zeros((cells, EDGE + 1))
    send_left[np.arange(EDGE), np.arange(EDGE)] = 1.0
    send_left[EDGE:, EDGE] = r ** (np.arange(EDGE, cells) + 1.0)
    from_right = np.concatenate(
        [both(ov - cells - k),
         np.concatenate([tail * r ** (cells - 1 - ov), tail * r ** (cells - 1 - ov) * (1.0 / r - r)], axis=-1)],
        axis=0,
    )
    return [np.asarray(t, np.float32) for t in (own, send_right, from_left, send_left, from_right)]


def neighbours(value, axis, wrap):
    size = lax.axis_size(axis)
    up = [(i, (i + 1) % size) for i in range(size if wrap else size - 1)]
    down = [(j, i) for i, j in up]
    return up, down


def shards(adjoint, coeff, flux, target_cell, donor_owner, donor_cell):
    fields, rows_x, rows_r, cells_a = adjoint.shape
    loop_span = cells_a * lax.axis_size("az")
    rows = rows_x * rows_r
    own_t, send_right_t, from_left_t, send_left_t, from_right_t = halo_tables(cells_a, loop_span)
    lines = adjoint.reshape(fields * rows, cells_a)

    up, down = neighbours(adjoint, "az", True)
    right_moment = jnp.asarray(send_right_t[:, EDGE])
    left_moment = jnp.asarray(send_left_t[:, EDGE])
    to_right = jnp.concatenate(
        [lines[:, cells_a - EDGE :], jnp.sum(lines * right_moment[None], axis=1, keepdims=True)], axis=1
    ).T
    to_left = jnp.concatenate(
        [lines[:, :EDGE], jnp.sum(lines * left_moment[None], axis=1, keepdims=True)], axis=1
    ).T
    from_left = lax.ppermute(to_right, "az", up)
    from_right = lax.ppermute(to_left, "az", down)
    both = jnp.einsum("lc,co->lo", lines, jnp.asarray(own_t), precision=HI)
    both = both + jnp.einsum("kl,ko->lo", from_left, jnp.asarray(from_left_t), precision=HI)
    both = both + jnp.einsum("kl,ko->lo", from_right, jnp.asarray(from_right_t), precision=HI)
    both = both.reshape(fields, rows_x, rows_r, 2 * cells_a)
    filtered = both[..., :cells_a]
    along_a = both[..., cells_a:]

    row_ids = jnp.arange(rows, dtype=jnp.int32)
    lane_ids = jnp.arange(cells_a, dtype=jnp.int32)
    t_rows = (target_cell[:, None] // cells_a == row_ids[None, :]).astype(jnp.float32)
    t_lanes = (target_cell[:, None] % cells_a == lane_ids[None, :]).astype(jnp.float32)
    flat = filtered.reshape(fields, rows, cells_a)
    picked = jnp.einsum("tk,fka->fta", t_rows, flat, precision=HI)
    source = sat_gain * jnp.sum(picked * t_lanes[None], axis=2)

    owner_rows = donor_owner[:, 0]
    owners = lax.axis_size("gx")
    capacity = target_cell.shape[0] // 8
    onehot = (owner_rows[:, None] == jnp.arange(owners, dtype=jnp.int32)[None, :]).astype(jnp.int32)
    slot_rank = jnp.sum(onehot * (jnp.cumsum(onehot, axis=0) - 1), axis=1)
    slot_place = owner_rows * capacity + slot_rank
    packed = jnp.concatenate([source, donor_cell.astype(jnp.float32)[None, :]], axis=0)
    slots = (
        slot_place[:, None, None]
        == (jnp.arange(owners, dtype=jnp.int32)[:, None] * capacity + jnp.arange(capacity, dtype=jnp.int32))[None]
    ).astype(jnp.float32)
    outbox = jnp.einsum("pt,tos->ops", packed, slots, precision=HI).reshape(owners, (fields + 1) * capacity)
    received = lax.all_to_all(outbox, "gx", split_axis=0, concat_axis=0, tiled=True)
    taken = jnp.einsum("nk,fna->fka", t_rows, -source[:, :, None] * t_lanes[None], precision=HI)
    up_x, down_x = neighbours(filtered, "gx", False)
    last_x, first_x, last_r, first_r, received = lax.optimization_barrier(
        (filtered[:, -1], filtered[:, 0], filtered[:, :, -1], filtered[:, :, 0], received)
    )
    before_x = lax.ppermute(last_x, "gx", up_x)[:, None]
    after_x = lax.ppermute(first_x, "gx", down_x)[:, None]
    if lax.axis_size("row") == 2:
        band = lax.axis_index("row")
        other = lax.ppermute(jnp.where(band == 0, last_r, first_r), "row", [(0, 1), (1, 0)])
        before_r = jnp.where(band == 1, other, 0.0)[:, :, None]
        after_r = jnp.where(band == 0, other, 0.0)[:, :, None]
    else:
        up_r, down_r = neighbours(filtered, "row", False)
        before_r = lax.ppermute(last_r, "row", up_r)[:, :, None]
        after_r = lax.ppermute(first_r, "row", down_r)[:, :, None]
    along_x = jnp.concatenate([filtered[:, 1:], after_x], axis=1) - jnp.concatenate(
        [before_x, filtered[:, :-1]], axis=1
    )
    along_r = jnp.concatenate([filtered[:, :, 1:], after_r], axis=2) - jnp.concatenate(
        [before_r, filtered[:, :, :-1]], axis=2
    )
    gradient = filtered
    for direction, change in enumerate((along_x, along_r, along_a)):
        mixing = jnp.einsum("fg,fxra->gxra", flux[direction], change, precision=HI)
        gradient = gradient + coeff[direction][None] * mixing
    gradient = gradient + taken.reshape(adjoint.shape)

    received = received.reshape(owners, fields + 1, capacity).transpose(1, 0, 2).reshape(fields + 1, owners * capacity)
    got_cell = received[fields].astype(jnp.int32)
    d_rows = (got_cell[:, None] // cells_a == row_ids[None, :]).astype(jnp.float32)
    d_lanes = (got_cell[:, None] % cells_a == lane_ids[None, :]).astype(jnp.float32)
    spread = received[:fields, :, None] * d_lanes[None]
    update = jnp.einsum("nk,fna->fka", d_rows, spread, precision=HI)
    return gradient + update.reshape(adjoint.shape)


def solution(mesh):
    return jax.shard_map(
        shards,
        mesh=mesh,
        in_specs=(
            P(None, "gx", "row", "az"),
            P(None, "gx", "row", "az"),
            P(),
            P(("gx", "az", "row")),
            P(("gx", "az", "row"), None),
            P(("gx", "az", "row")),
        ),
        out_specs=P(None, "gx", "row", "az"),
        check_vma=False,
    )
```

```python
import jax
import jax.numpy as jnp
import numpy as np
from jax import lax
from jax.sharding import PartitionSpec as P

filter_alpha = 0.49
sat_gain = 0.5
pade_coeffs = [
    (193.0 + 126.0 * filter_alpha) / 256.0,
    (105.0 + 302.0 * filter_alpha) / 256.0,
    15.0 * (2.0 * filter_alpha - 1.0) / 64.0,
    45.0 * (1.0 - 2.0 * filter_alpha) / 512.0,
    5.0 * (2.0 * filter_alpha - 1.0) / 256.0,
    (1.0 - 2.0 * filter_alpha) / 512.0,
]
HI = lax.Precision.HIGHEST


root_value = (-1.0 + (1.0 - 4.0 * filter_alpha * filter_alpha) ** 0.5) / (2.0 * filter_alpha)
green_scale = 1.0 / (1.0 + 2.0 * filter_alpha * root_value)
EDGE = 7


def stencil_weight(shift):
    return pade_coeffs[0] if shift == 0 else 0.5 * pade_coeffs[abs(shift)]


def loop_weight(offset, length):
    total = np.zeros(np.shape(offset))
    for shift in range(-5, 6):
        n = np.mod(offset - shift, length)
        images = root_value ** n + root_value ** (length - n)
        total = total + stencil_weight(shift) * green_scale * images / (1.0 - root_value**length)
    return total


def halo_tables(cells, length):
    r = root_value
    tail = green_scale / (1.0 - r**length) * sum(stencil_weight(s) * r ** (-s) for s in range(-5, 6))
    c = np.arange(cells)[:, None]
    o = np.arange(cells)[None, :]

    def both(distance):
        return np.concatenate(
            [loop_weight(distance, length), loop_weight(distance + 1, length) - loop_weight(distance - 1, length)],
            axis=-1,
        )

    own = both(o - c)
    k = np.arange(EDGE)[:, None]
    ov = np.arange(cells)[None, :]
    send_right = np.zeros((cells, EDGE + 1))
    send_right[cells - EDGE + np.arange(EDGE), np.arange(EDGE)] = 1.0
    send_right[: cells - EDGE, EDGE] = r ** (cells - np.arange(cells - EDGE))
    from_left = np.concatenate(
        [both(ov + cells - (cells - EDGE + k)),
         np.concatenate([tail * r**ov, tail * r**ov * (r - 1.0 / r)], axis=-1)],
        axis=0,
    )
    send_left = np.zeros((cells, EDGE + 1))
    send_left[np.arange(EDGE), np.arange(EDGE)] = 1.0
    send_left[EDGE:, EDGE] = r ** (np.arange(EDGE, cells) + 1.0)
    from_right = np.concatenate(
        [both(ov - cells - k),
         np.concatenate([tail * r ** (cells - 1 - ov), tail * r ** (cells - 1 - ov) * (1.0 / r - r)], axis=-1)],
        axis=0,
    )
    return [np.asarray(t, np.float32) for t in (own, send_right, from_left, send_left, from_right)]


def neighbours(value, axis, wrap):
    size = lax.axis_size(axis)
    up = [(i, (i + 1) % size) for i in range(size if wrap else size - 1)]
    down = [(j, i) for i, j in up]
    return up, down


def shards(adjoint, coeff, flux, target_cell, donor_owner, donor_cell):
    fields, rows_x, rows_r, cells_a = adjoint.shape
    loop_span = cells_a * lax.axis_size("az")
    rows = rows_x * rows_r
    own_t, send_right_t, from_left_t, send_left_t, from_right_t = halo_tables(cells_a, loop_span)
    lines = adjoint.reshape(fields * rows, cells_a)

    up, down = neighbours(adjoint, "az", True)
    right_moment = jnp.asarray(send_right_t[:, EDGE])
    left_moment = jnp.asarray(send_left_t[:, EDGE])
    to_right = jnp.concatenate(
        [lines[:, cells_a - EDGE :], jnp.sum(lines * right_moment[None], axis=1, keepdims=True)], axis=1
    ).T
    to_left = jnp.concatenate(
        [lines[:, :EDGE], jnp.sum(lines * left_moment[None], axis=1, keepdims=True)], axis=1
    ).T
    from_left = lax.ppermute(to_right, "az", up)
    from_right = lax.ppermute(to_left, "az", down)
    both = jnp.einsum("lc,co->lo", lines, jnp.asarray(own_t), precision=HI)
    both = both + jnp.einsum("kl,ko->lo", from_left, jnp.asarray(from_left_t), precision=HI)
    both = both + jnp.einsum("kl,ko->lo", from_right, jnp.asarray(from_right_t), precision=HI)
    both = both.reshape(fields, rows_x, rows_r, 2 * cells_a)
    filtered = both[..., :cells_a]
    along_a = both[..., cells_a:]

    row_ids = jnp.arange(rows, dtype=jnp.int32)
    lane_ids = jnp.arange(cells_a, dtype=jnp.int32)
    t_rows = (target_cell[:, None] // cells_a == row_ids[None, :]).astype(jnp.float32)
    t_lanes = (target_cell[:, None] % cells_a == lane_ids[None, :]).astype(jnp.float32)
    flat = filtered.reshape(fields, rows, cells_a)
    picked = jnp.einsum("tk,fka->fta", t_rows, flat, precision=HI)
    source = sat_gain * jnp.sum(picked * t_lanes[None], axis=2)

    owner_rows = donor_owner[:, 0]
    owners = lax.axis_size("gx")
    capacity = target_cell.shape[0] // 8
    onehot = (owner_rows[:, None] == jnp.arange(owners, dtype=jnp.int32)[None, :]).astype(jnp.int32)
    slot_rank = jnp.sum(onehot * (jnp.cumsum(onehot, axis=0) - 1), axis=1)
    slot_place = owner_rows * capacity + slot_rank
    packed = jnp.concatenate([source, donor_cell.astype(jnp.float32)[None, :]], axis=0)
    by_rank = (slot_rank[None, :] == jnp.arange(capacity, dtype=jnp.int32)[:, None]).astype(jnp.float32)
    spread_out = (packed[:, None, :] * by_rank[None]).reshape((fields + 1) * capacity, -1)
    outbox = jnp.einsum("qt,to->oq", spread_out, onehot.astype(jnp.float32), precision=HI)
    received = lax.all_to_all(outbox, "gx", split_axis=0, concat_axis=0, tiled=True)
    taken = jnp.einsum("nk,fna->fka", t_rows, -source[:, :, None] * t_lanes[None], precision=HI)
    up_x, down_x = neighbours(filtered, "gx", False)
    last_x, first_x, last_r, first_r = filtered[:, -1], filtered[:, 0], filtered[:, :, -1], filtered[:, :, 0]
    before_x = lax.ppermute(last_x, "gx", up_x)[:, None]
    after_x = lax.ppermute(first_x, "gx", down_x)[:, None]
    if lax.axis_size("row") == 2:
        band = lax.axis_index("row")
        other = lax.ppermute(jnp.where(band == 0, last_r, first_r), "row", [(0, 1), (1, 0)])
        before_r = jnp.where(band == 1, other, 0.0)[:, :, None]
        after_r = jnp.where(band == 0, other, 0.0)[:, :, None]
    else:
        up_r, down_r = neighbours(filtered, "row", False)
        before_r = lax.ppermute(last_r, "row", up_r)[:, :, None]
        after_r = lax.ppermute(first_r, "row", down_r)[:, :, None]
    along_x = jnp.concatenate([filtered[:, 1:], after_x], axis=1) - jnp.concatenate(
        [before_x, filtered[:, :-1]], axis=1
    )
    along_r = jnp.concatenate([filtered[:, :, 1:], after_r], axis=2) - jnp.concatenate(
        [before_r, filtered[:, :, :-1]], axis=2
    )
    changes = (along_x, along_r, along_a)
    out_fields = []
    for g in range(fields):
        total = filtered[g] + taken[g].reshape(rows_x, rows_r, cells_a)
        for direction, change in enumerate(changes):
            mixing = flux[direction, 0, g] * change[0]
            for f in range(1, fields):
                mixing = mixing + flux[direction, f, g] * change[f]
            total = total + coeff[direction] * mixing
        out_fields.append(total)
    gradient = jnp.stack(out_fields)

    received = received.reshape(owners, fields + 1, capacity).transpose(1, 0, 2).reshape(fields + 1, owners * capacity)
    got_cell = received[fields].astype(jnp.int32)
    d_rows = (got_cell[:, None] // cells_a == row_ids[None, :]).astype(jnp.float32)
    d_lanes = (got_cell[:, None] % cells_a == lane_ids[None, :]).astype(jnp.float32)
    spread = received[:fields, :, None] * d_lanes[None]
    update = jnp.einsum("nk,fna->fka", d_rows, spread, precision=HI)
    return gradient + update.reshape(adjoint.shape)


def solution(mesh):
    return jax.shard_map(
        shards,
        mesh=mesh,
        in_specs=(
            P(None, "gx", "row", "az"),
            P(None, "gx", "row", "az"),
            P(),
            P(("gx", "az", "row")),
            P(("gx", "az", "row"), None),
            P(("gx", "az", "row")),
        ),
        out_specs=P(None, "gx", "row", "az"),
        check_vma=False,
    )
```

```python
import jax
import jax.numpy as jnp
import numpy as np
from jax import lax
from jax.sharding import PartitionSpec as P

filter_alpha = 0.49
sat_gain = 0.5
pade_coeffs = [
    (193.0 + 126.0 * filter_alpha) / 256.0,
    (105.0 + 302.0 * filter_alpha) / 256.0,
    15.0 * (2.0 * filter_alpha - 1.0) / 64.0,
    45.0 * (1.0 - 2.0 * filter_alpha) / 512.0,
    5.0 * (2.0 * filter_alpha - 1.0) / 256.0,
    (1.0 - 2.0 * filter_alpha) / 512.0,
]
HI = lax.Precision.HIGHEST


root_value = (-1.0 + (1.0 - 4.0 * filter_alpha * filter_alpha) ** 0.5) / (2.0 * filter_alpha)
green_scale = 1.0 / (1.0 + 2.0 * filter_alpha * root_value)
EDGE = 7


def stencil_weight(shift):
    return pade_coeffs[0] if shift == 0 else 0.5 * pade_coeffs[abs(shift)]


def loop_weight(offset, length):
    total = np.zeros(np.shape(offset))
    for shift in range(-5, 6):
        n = np.mod(offset - shift, length)
        images = root_value ** n + root_value ** (length - n)
        total = total + stencil_weight(shift) * green_scale * images / (1.0 - root_value**length)
    return total


def halo_tables(cells, length):
    r = root_value
    tail = green_scale / (1.0 - r**length) * sum(stencil_weight(s) * r ** (-s) for s in range(-5, 6))
    c = np.arange(cells)[:, None]
    o = np.arange(cells)[None, :]

    def both(distance):
        return np.concatenate(
            [loop_weight(distance, length), loop_weight(distance + 1, length) - loop_weight(distance - 1, length)],
            axis=-1,
        )

    own = both(o - c)
    k = np.arange(EDGE)[:, None]
    ov = np.arange(cells)[None, :]
    send_right = np.zeros((cells, EDGE + 1))
    send_right[cells - EDGE + np.arange(EDGE), np.arange(EDGE)] = 1.0
    send_right[: cells - EDGE, EDGE] = r ** (cells - np.arange(cells - EDGE))
    from_left = np.concatenate(
        [both(ov + cells - (cells - EDGE + k)),
         np.concatenate([tail * r**ov, tail * r**ov * (r - 1.0 / r)], axis=-1)],
        axis=0,
    )
    send_left = np.zeros((cells, EDGE + 1))
    send_left[np.arange(EDGE), np.arange(EDGE)] = 1.0
    send_left[EDGE:, EDGE] = r ** (np.arange(EDGE, cells) + 1.0)
    from_right = np.concatenate(
        [both(ov - cells - k),
         np.concatenate([tail * r ** (cells - 1 - ov), tail * r ** (cells - 1 - ov) * (1.0 / r - r)], axis=-1)],
        axis=0,
    )
    return [np.asarray(t, np.float32) for t in (own, send_right, from_left, send_left, from_right)]


def neighbours(value, axis, wrap):
    size = lax.axis_size(axis)
    up = [(i, (i + 1) % size) for i in range(size if wrap else size - 1)]
    down = [(j, i) for i, j in up]
    return up, down


def shards(adjoint, coeff, flux, target_cell, donor_owner, donor_cell):
    fields, rows_x, rows_r, cells_a = adjoint.shape
    loop_span = cells_a * lax.axis_size("az")
    rows = rows_x * rows_r
    own_t, send_right_t, from_left_t, send_left_t, from_right_t = halo_tables(cells_a, loop_span)
    lines = adjoint.reshape(fields * rows, cells_a)

    up, down = neighbours(adjoint, "az", True)
    right_moment = jnp.asarray(send_right_t[:, EDGE])
    left_moment = jnp.asarray(send_left_t[:, EDGE])
    to_right = jnp.concatenate(
        [lines[:, cells_a - EDGE :], jnp.sum(lines * right_moment[None], axis=1, keepdims=True)], axis=1
    ).T
    to_left = jnp.concatenate(
        [lines[:, :EDGE], jnp.sum(lines * left_moment[None], axis=1, keepdims=True)], axis=1
    ).T
    from_left = lax.ppermute(to_right, "az", up)
    from_right = lax.ppermute(to_left, "az", down)
    both = jnp.einsum("lc,co->lo", lines, jnp.asarray(own_t), precision=HI)
    both = both + jnp.einsum("kl,ko->lo", from_left, jnp.asarray(from_left_t), precision=HI)
    both = both + jnp.einsum("kl,ko->lo", from_right, jnp.asarray(from_right_t), precision=HI)
    both = both.reshape(fields, rows_x, rows_r, 2 * cells_a)
    filtered = both[..., :cells_a]
    along_a = both[..., cells_a:]

    row_ids = jnp.arange(rows, dtype=jnp.int32)
    lane_ids = jnp.arange(cells_a, dtype=jnp.int32)
    t_rows = (target_cell[:, None] // cells_a == row_ids[None, :]).astype(jnp.float32)
    t_lanes = (target_cell[:, None] % cells_a == lane_ids[None, :]).astype(jnp.float32)
    flat = filtered.reshape(fields, rows, cells_a)
    picked = jnp.einsum("tk,fka->fta", t_rows, flat, precision=HI)
    source = sat_gain * jnp.sum(picked * t_lanes[None], axis=2)

    owner_rows = donor_owner[:, 0]
    owners = lax.axis_size("gx")
    capacity = target_cell.shape[0] // 8
    onehot = (owner_rows[:, None] == jnp.arange(owners, dtype=jnp.int32)[None, :]).astype(jnp.int32)
    slot_rank = jnp.sum(onehot * (jnp.cumsum(onehot, axis=0) - 1), axis=1)
    slot_place = owner_rows * capacity + slot_rank
    packed = jnp.concatenate([source, donor_cell.astype(jnp.float32)[None, :]], axis=0)
    by_rank = (slot_rank[None, :] == jnp.arange(capacity, dtype=jnp.int32)[:, None]).astype(jnp.float32)
    spread_out = (packed[:, None, :] * by_rank[None]).reshape((fields + 1) * capacity, -1)
    outbox = jnp.einsum("qt,to->oq", spread_out, onehot.astype(jnp.float32), precision=HI)
    received = lax.all_to_all(outbox, "gx", split_axis=0, concat_axis=0, tiled=True)
    taken = jnp.einsum("nk,fna->fka", t_rows, -source[:, :, None] * t_lanes[None], precision=HI)
    up_x, down_x = neighbours(filtered, "gx", False)
    last_x, first_x, last_r, first_r = filtered[:, -1], filtered[:, 0], filtered[:, :, -1], filtered[:, :, 0]
    before_x = lax.ppermute(last_x, "gx", up_x)[:, None]
    after_x = lax.ppermute(first_x, "gx", down_x)[:, None]
    if lax.axis_size("row") == 2:
        band = lax.axis_index("row")
        other = lax.ppermute(jnp.where(band == 0, last_r, first_r), "row", [(0, 1), (1, 0)])
        before_r = jnp.where(band == 1, other, 0.0)[:, :, None]
        after_r = jnp.where(band == 0, other, 0.0)[:, :, None]
    else:
        up_r, down_r = neighbours(filtered, "row", False)
        before_r = lax.ppermute(last_r, "row", up_r)[:, :, None]
        after_r = lax.ppermute(first_r, "row", down_r)[:, :, None]
    along_x = jnp.concatenate([filtered[:, 1:], after_x], axis=1) - jnp.concatenate(
        [before_x, filtered[:, :-1]], axis=1
    )
    along_r = jnp.concatenate([filtered[:, :, 1:], after_r], axis=2) - jnp.concatenate(
        [before_r, filtered[:, :, :-1]], axis=2
    )
    gradient = filtered
    for direction, change in enumerate((along_x, along_r, along_a)):
        mixing = jnp.einsum("fg,fxra->gxra", flux[direction], change, precision=HI)
        gradient = gradient + coeff[direction][None] * mixing
    gradient = gradient + taken.reshape(adjoint.shape)

    received = received.reshape(owners, fields + 1, capacity).transpose(1, 0, 2).reshape(fields + 1, owners * capacity)
    got_cell = received[fields].astype(jnp.int32)
    d_rows = (got_cell[:, None] // cells_a == row_ids[None, :]).astype(jnp.float32)
    d_lanes = (got_cell[:, None] % cells_a == lane_ids[None, :]).astype(jnp.float32)
    spread = received[:fields, :, None] * d_lanes[None]
    update = jnp.einsum("nk,fna->fka", d_rows, spread, precision=HI)
    return gradient + update.reshape(adjoint.shape)


def solution(mesh):
    return jax.shard_map(
        shards,
        mesh=mesh,
        in_specs=(
            P(None, "gx", "row", "az"),
            P(None, "gx", "row", "az"),
            P(),
            P(("gx", "az", "row")),
            P(("gx", "az", "row"), None),
            P(("gx", "az", "row")),
        ),
        out_specs=P(None, "gx", "row", "az"),
        check_vma=False,
    )
```

```python
import jax
import jax.numpy as jnp
import numpy as np
from jax import lax
from jax.sharding import PartitionSpec as P

filter_alpha = 0.49
sat_gain = 0.5
pade_coeffs = [
    (193.0 + 126.0 * filter_alpha) / 256.0,
    (105.0 + 302.0 * filter_alpha) / 256.0,
    15.0 * (2.0 * filter_alpha - 1.0) / 64.0,
    45.0 * (1.0 - 2.0 * filter_alpha) / 512.0,
    5.0 * (2.0 * filter_alpha - 1.0) / 256.0,
    (1.0 - 2.0 * filter_alpha) / 512.0,
]
HI = lax.Precision.HIGHEST


root_value = (-1.0 + (1.0 - 4.0 * filter_alpha * filter_alpha) ** 0.5) / (2.0 * filter_alpha)
green_scale = 1.0 / (1.0 + 2.0 * filter_alpha * root_value)
EDGE = 7


def stencil_weight(shift):
    return pade_coeffs[0] if shift == 0 else 0.5 * pade_coeffs[abs(shift)]


def loop_weight(offset, length):
    total = np.zeros(np.shape(offset))
    for shift in range(-5, 6):
        n = np.mod(offset - shift, length)
        images = root_value ** n + root_value ** (length - n)
        total = total + stencil_weight(shift) * green_scale * images / (1.0 - root_value**length)
    return total


def halo_tables(cells, length):
    r = root_value
    tail = green_scale / (1.0 - r**length) * sum(stencil_weight(s) * r ** (-s) for s in range(-5, 6))
    c = np.arange(cells)[:, None]
    o = np.arange(cells)[None, :]

    def both(distance):
        return np.concatenate(
            [loop_weight(distance, length), loop_weight(distance + 1, length) - loop_weight(distance - 1, length)],
            axis=-1,
        )

    own = both(o - c)
    k = np.arange(EDGE)[:, None]
    ov = np.arange(cells)[None, :]
    send_right = np.zeros((cells, EDGE + 1))
    send_right[cells - EDGE + np.arange(EDGE), np.arange(EDGE)] = 1.0
    send_right[: cells - EDGE, EDGE] = r ** (cells - np.arange(cells - EDGE))
    from_left = np.concatenate(
        [both(ov + cells - (cells - EDGE + k)),
         np.concatenate([tail * r**ov, tail * r**ov * (r - 1.0 / r)], axis=-1)],
        axis=0,
    )
    send_left = np.zeros((cells, EDGE + 1))
    send_left[np.arange(EDGE), np.arange(EDGE)] = 1.0
    send_left[EDGE:, EDGE] = r ** (np.arange(EDGE, cells) + 1.0)
    from_right = np.concatenate(
        [both(ov - cells - k),
         np.concatenate([tail * r ** (cells - 1 - ov), tail * r ** (cells - 1 - ov) * (1.0 / r - r)], axis=-1)],
        axis=0,
    )
    return [np.asarray(t, np.float32) for t in (own, send_right, from_left, send_left, from_right)]


def neighbours(value, axis, wrap):
    size = lax.axis_size(axis)
    up = [(i, (i + 1) % size) for i in range(size if wrap else size - 1)]
    down = [(j, i) for i, j in up]
    return up, down


def shards(adjoint, coeff, flux, target_cell, donor_owner, donor_cell):
    fields, rows_x, rows_r, cells_a = adjoint.shape
    loop_span = cells_a * lax.axis_size("az")
    rows = rows_x * rows_r
    own_t, send_right_t, from_left_t, send_left_t, from_right_t = halo_tables(cells_a, loop_span)
    lines = adjoint.reshape(fields * rows, cells_a)

    up, down = neighbours(adjoint, "az", True)
    right_moment = jnp.asarray(send_right_t[:, EDGE])
    left_moment = jnp.asarray(send_left_t[:, EDGE])
    to_right = jnp.concatenate(
        [lines[:, cells_a - EDGE :], jnp.sum(lines * right_moment[None], axis=1, keepdims=True)], axis=1
    ).T
    to_left = jnp.concatenate(
        [lines[:, :EDGE], jnp.sum(lines * left_moment[None], axis=1, keepdims=True)], axis=1
    ).T
    from_left = lax.ppermute(to_right, "az", up)
    from_right = lax.ppermute(to_left, "az", down)
    both = jnp.einsum("lc,co->lo", lines, jnp.asarray(own_t), precision=HI)
    both = both + jnp.einsum("kl,ko->lo", from_left, jnp.asarray(from_left_t), precision=HI)
    both = both + jnp.einsum("kl,ko->lo", from_right, jnp.asarray(from_right_t), precision=HI)
    both = both.reshape(fields, rows_x, rows_r, 2 * cells_a)
    filtered = both[..., :cells_a]
    along_a = both[..., cells_a:]

    row_ids = jnp.arange(rows, dtype=jnp.int32)
    lane_ids = jnp.arange(cells_a, dtype=jnp.int32)
    t_rows = (target_cell[:, None] // cells_a == row_ids[None, :]).astype(jnp.float32)
    t_lanes = (target_cell[:, None] % cells_a == lane_ids[None, :]).astype(jnp.float32)
    flat = filtered.reshape(fields, rows, cells_a)
    picked = jnp.einsum("tk,fka->fta", t_rows, flat, precision=HI)
    source = sat_gain * jnp.sum(picked * t_lanes[None], axis=2)

    owner_rows = donor_owner[:, 0]
    owners = lax.axis_size("gx")
    capacity = target_cell.shape[0] // 8
    onehot = (owner_rows[:, None] == jnp.arange(owners, dtype=jnp.int32)[None, :]).astype(jnp.int32)
    slot_rank = jnp.sum(onehot * (jnp.cumsum(onehot, axis=0) - 1), axis=1)
    slot_place = owner_rows * capacity + slot_rank
    packed = jnp.concatenate([source, donor_cell.astype(jnp.float32)[None, :]], axis=0)
    by_rank = (slot_rank[None, :] == jnp.arange(capacity, dtype=jnp.int32)[:, None]).astype(jnp.float32)
    spread_out = (packed[:, None, :] * by_rank[None]).reshape((fields + 1) * capacity, -1)
    outbox = jnp.einsum("qt,to->oq", spread_out, onehot.astype(jnp.float32), precision=HI)
    received = lax.all_to_all(outbox, "gx", split_axis=0, concat_axis=0, tiled=True)
    taken = jnp.einsum("nk,fna->fka", t_rows, -source[:, :, None] * t_lanes[None], precision=HI)
    up_x, down_x = neighbours(filtered, "gx", False)
    last_x, first_x, last_r, first_r = filtered[:, -1], filtered[:, 0], filtered[:, :, -1], filtered[:, :, 0]
    before_x = lax.ppermute(last_x, "gx", up_x)[:, None]
    after_x = lax.ppermute(first_x, "gx", down_x)[:, None]
    if lax.axis_size("row") == 2:
        band = lax.axis_index("row")
        other = lax.ppermute(jnp.where(band == 0, last_r, first_r), "row", [(0, 1), (1, 0)])
        before_r = jnp.where(band == 1, other, 0.0)[:, :, None]
        after_r = jnp.where(band == 0, other, 0.0)[:, :, None]
    else:
        up_r, down_r = neighbours(filtered, "row", False)
        before_r = lax.ppermute(last_r, "row", up_r)[:, :, None]
        after_r = lax.ppermute(first_r, "row", down_r)[:, :, None]
    along_x = jnp.concatenate([filtered[:, 1:], after_x], axis=1) - jnp.concatenate(
        [before_x, filtered[:, :-1]], axis=1
    )
    along_r = jnp.concatenate([filtered[:, :, 1:], after_r], axis=2) - jnp.concatenate(
        [before_r, filtered[:, :, :-1]], axis=2
    )
    changes = lax.optimization_barrier((along_x, along_r, along_a))
    gradient = filtered + taken.reshape(adjoint.shape)
    for direction, change in enumerate(changes):
        mixing = flux[direction, 0][:, None, None, None] * change[0][None]
        for f in range(1, fields):
            mixing = mixing + flux[direction, f][:, None, None, None] * change[f][None]
        gradient = gradient + coeff[direction][None] * mixing
    gradient, received = lax.optimization_barrier((gradient, received))

    received = received.reshape(owners, fields + 1, capacity).transpose(1, 0, 2).reshape(fields + 1, owners * capacity)
    got_cell = received[fields].astype(jnp.int32)
    d_rows = (got_cell[:, None] // cells_a == row_ids[None, :]).astype(jnp.float32)
    d_lanes = (got_cell[:, None] % cells_a == lane_ids[None, :]).astype(jnp.float32)
    spread = received[:fields, :, None] * d_lanes[None]
    update = jnp.einsum("nk,fna->fka", d_rows, spread, precision=HI)
    return gradient + update.reshape(adjoint.shape)


def solution(mesh):
    return jax.shard_map(
        shards,
        mesh=mesh,
        in_specs=(
            P(None, "gx", "row", "az"),
            P(None, "gx", "row", "az"),
            P(),
            P(("gx", "az", "row")),
            P(("gx", "az", "row"), None),
            P(("gx", "az", "row")),
        ),
        out_specs=P(None, "gx", "row", "az"),
        check_vma=False,
    )
```

```python
import jax
import jax.numpy as jnp
import numpy as np
from jax import lax
from jax.sharding import PartitionSpec as P

filter_alpha = 0.49
sat_gain = 0.5
pade_coeffs = [
    (193.0 + 126.0 * filter_alpha) / 256.0,
    (105.0 + 302.0 * filter_alpha) / 256.0,
    15.0 * (2.0 * filter_alpha - 1.0) / 64.0,
    45.0 * (1.0 - 2.0 * filter_alpha) / 512.0,
    5.0 * (2.0 * filter_alpha - 1.0) / 256.0,
    (1.0 - 2.0 * filter_alpha) / 512.0,
]
HI = lax.Precision.HIGHEST


root_value = (-1.0 + (1.0 - 4.0 * filter_alpha * filter_alpha) ** 0.5) / (2.0 * filter_alpha)
green_scale = 1.0 / (1.0 + 2.0 * filter_alpha * root_value)
EDGE = 7


def stencil_weight(shift):
    return pade_coeffs[0] if shift == 0 else 0.5 * pade_coeffs[abs(shift)]


def loop_weight(offset, length):
    total = np.zeros(np.shape(offset))
    for shift in range(-5, 6):
        n = np.mod(offset - shift, length)
        images = root_value ** n + root_value ** (length - n)
        total = total + stencil_weight(shift) * green_scale * images / (1.0 - root_value**length)
    return total


def halo_tables(cells, length):
    r = root_value
    tail = green_scale / (1.0 - r**length) * sum(stencil_weight(s) * r ** (-s) for s in range(-5, 6))
    c = np.arange(cells)[:, None]
    o = np.arange(cells)[None, :]

    def both(distance):
        return np.concatenate(
            [loop_weight(distance, length), loop_weight(distance + 1, length) - loop_weight(distance - 1, length)],
            axis=-1,
        )

    own = both(o - c)
    k = np.arange(EDGE)[:, None]
    ov = np.arange(cells)[None, :]
    send_right = np.zeros((cells, EDGE + 1))
    send_right[cells - EDGE + np.arange(EDGE), np.arange(EDGE)] = 1.0
    send_right[: cells - EDGE, EDGE] = r ** (cells - np.arange(cells - EDGE))
    from_left = np.concatenate(
        [both(ov + cells - (cells - EDGE + k)),
         np.concatenate([tail * r**ov, tail * r**ov * (r - 1.0 / r)], axis=-1)],
        axis=0,
    )
    send_left = np.zeros((cells, EDGE + 1))
    send_left[np.arange(EDGE), np.arange(EDGE)] = 1.0
    send_left[EDGE:, EDGE] = r ** (np.arange(EDGE, cells) + 1.0)
    from_right = np.concatenate(
        [both(ov - cells - k),
         np.concatenate([tail * r ** (cells - 1 - ov), tail * r ** (cells - 1 - ov) * (1.0 / r - r)], axis=-1)],
        axis=0,
    )
    return [np.asarray(t, np.float32) for t in (own, send_right, from_left, send_left, from_right)]


def neighbours(value, axis, wrap):
    size = lax.axis_size(axis)
    up = [(i, (i + 1) % size) for i in range(size if wrap else size - 1)]
    down = [(j, i) for i, j in up]
    return up, down


def shards(adjoint, coeff, flux, target_cell, donor_owner, donor_cell):
    fields, rows_x, rows_r, cells_a = adjoint.shape
    loop_span = cells_a * lax.axis_size("az")
    rows = rows_x * rows_r
    own_t, send_right_t, from_left_t, send_left_t, from_right_t = halo_tables(cells_a, loop_span)
    lines = adjoint.reshape(fields * rows, cells_a)

    up, down = neighbours(adjoint, "az", True)
    selector = jnp.asarray(np.concatenate([send_right_t, send_left_t], axis=1).T)
    payload = jnp.einsum("kc,lc->kl", selector, lines, precision=HI)
    to_right, to_left = payload[: EDGE + 1], payload[EDGE + 1 :]
    from_left = lax.ppermute(to_right, "az", up)
    from_right = lax.ppermute(to_left, "az", down)
    both = jnp.einsum("lc,co->lo", lines, jnp.asarray(own_t), precision=HI)
    both = both + jnp.einsum("kl,ko->lo", from_left, jnp.asarray(from_left_t), precision=HI)
    both = both + jnp.einsum("kl,ko->lo", from_right, jnp.asarray(from_right_t), precision=HI)
    both = both.reshape(fields, rows_x, rows_r, 2 * cells_a)
    filtered = both[..., :cells_a]
    along_a = both[..., cells_a:]

    row_ids = jnp.arange(rows, dtype=jnp.int32)
    lane_ids = jnp.arange(cells_a, dtype=jnp.int32)
    t_rows = (target_cell[:, None] // cells_a == row_ids[None, :]).astype(jnp.float32)
    t_lanes = (target_cell[:, None] % cells_a == lane_ids[None, :]).astype(jnp.float32)
    flat = filtered.reshape(fields, rows, cells_a)
    picked = jnp.einsum("tk,fka->fta", t_rows, flat, precision=HI)
    source = sat_gain * jnp.sum(picked * t_lanes[None], axis=2)

    owner_rows = donor_owner[:, 0]
    owners = lax.axis_size("gx")
    capacity = target_cell.shape[0] // 8
    onehot = (owner_rows[:, None] == jnp.arange(owners, dtype=jnp.int32)[None, :]).astype(jnp.int32)
    slot_rank = jnp.sum(onehot * (jnp.cumsum(onehot, axis=0) - 1), axis=1)
    slot_place = owner_rows * capacity + slot_rank
    packed = jnp.concatenate([source, donor_cell.astype(jnp.float32)[None, :]], axis=0)
    by_rank = (slot_rank[None, :] == jnp.arange(capacity, dtype=jnp.int32)[:, None]).astype(jnp.float32)
    spread_out = (packed[:, None, :] * by_rank[None]).reshape((fields + 1) * capacity, -1)
    outbox = jnp.einsum("qt,to->oq", spread_out, onehot.astype(jnp.float32), precision=HI)
    received = lax.all_to_all(outbox, "gx", split_axis=0, concat_axis=0, tiled=True)
    taken = jnp.einsum("nk,fna->fka", t_rows, -source[:, :, None] * t_lanes[None], precision=HI)
    up_x, down_x = neighbours(filtered, "gx", False)
    last_x, first_x, last_r, first_r = filtered[:, -1], filtered[:, 0], filtered[:, :, -1], filtered[:, :, 0]
    before_x = lax.ppermute(last_x, "gx", up_x)[:, None]
    after_x = lax.ppermute(first_x, "gx", down_x)[:, None]
    if lax.axis_size("row") == 2:
        band = lax.axis_index("row")
        other = lax.ppermute(jnp.where(band == 0, last_r, first_r), "row", [(0, 1), (1, 0)])
        before_r = jnp.where(band == 1, other, 0.0)[:, :, None]
        after_r = jnp.where(band == 0, other, 0.0)[:, :, None]
    else:
        up_r, down_r = neighbours(filtered, "row", False)
        before_r = lax.ppermute(last_r, "row", up_r)[:, :, None]
        after_r = lax.ppermute(first_r, "row", down_r)[:, :, None]
    along_x = jnp.concatenate([filtered[:, 1:], after_x], axis=1) - jnp.concatenate(
        [before_x, filtered[:, :-1]], axis=1
    )
    along_r = jnp.concatenate([filtered[:, :, 1:], after_r], axis=2) - jnp.concatenate(
        [before_r, filtered[:, :, :-1]], axis=2
    )
    changes = lax.optimization_barrier((along_x, along_r, along_a))
    gradient = filtered + taken.reshape(adjoint.shape)
    for direction, change in enumerate(changes):
        mixing = flux[direction, 0][:, None, None, None] * change[0][None]
        for f in range(1, fields):
            mixing = mixing + flux[direction, f][:, None, None, None] * change[f][None]
        gradient = gradient + coeff[direction][None] * mixing
    gradient, received = lax.optimization_barrier((gradient, received))

    received = received.reshape(owners, fields + 1, capacity).transpose(1, 0, 2).reshape(fields + 1, owners * capacity)
    got_cell = received[fields].astype(jnp.int32)
    d_rows = (got_cell[:, None] // cells_a == row_ids[None, :]).astype(jnp.float32)
    d_lanes = (got_cell[:, None] % cells_a == lane_ids[None, :]).astype(jnp.float32)
    spread = received[:fields, :, None] * d_lanes[None]
    update = jnp.einsum("nk,fna->fka", d_rows, spread, precision=HI)
    return gradient + update.reshape(adjoint.shape)


def solution(mesh):
    return jax.shard_map(
        shards,
        mesh=mesh,
        in_specs=(
            P(None, "gx", "row", "az"),
            P(None, "gx", "row", "az"),
            P(),
            P(("gx", "az", "row")),
            P(("gx", "az", "row"), None),
            P(("gx", "az", "row")),
        ),
        out_specs=P(None, "gx", "row", "az"),
        check_vma=False,
    )
```

```python
import jax
import jax.numpy as jnp
import numpy as np
from jax import lax
from jax.sharding import PartitionSpec as P

filter_alpha = 0.49
sat_gain = 0.5
pade_coeffs = [
    (193.0 + 126.0 * filter_alpha) / 256.0,
    (105.0 + 302.0 * filter_alpha) / 256.0,
    15.0 * (2.0 * filter_alpha - 1.0) / 64.0,
    45.0 * (1.0 - 2.0 * filter_alpha) / 512.0,
    5.0 * (2.0 * filter_alpha - 1.0) / 256.0,
    (1.0 - 2.0 * filter_alpha) / 512.0,
]
HI = lax.Precision.HIGH


root_value = (-1.0 + (1.0 - 4.0 * filter_alpha * filter_alpha) ** 0.5) / (2.0 * filter_alpha)
green_scale = 1.0 / (1.0 + 2.0 * filter_alpha * root_value)
EDGE = 7


def stencil_weight(shift):
    return pade_coeffs[0] if shift == 0 else 0.5 * pade_coeffs[abs(shift)]


def loop_weight(offset, length):
    total = np.zeros(np.shape(offset))
    for shift in range(-5, 6):
        n = np.mod(offset - shift, length)
        images = root_value ** n + root_value ** (length - n)
        total = total + stencil_weight(shift) * green_scale * images / (1.0 - root_value**length)
    return total


def halo_tables(cells, length):
    r = root_value
    tail = green_scale / (1.0 - r**length) * sum(stencil_weight(s) * r ** (-s) for s in range(-5, 6))
    c = np.arange(cells)[:, None]
    o = np.arange(cells)[None, :]

    def both(distance):
        return np.concatenate(
            [loop_weight(distance, length), loop_weight(distance + 1, length) - loop_weight(distance - 1, length)],
            axis=-1,
        )

    own = both(o - c)
    k = np.arange(EDGE)[:, None]
    ov = np.arange(cells)[None, :]
    send_right = np.zeros((cells, EDGE + 1))
    send_right[cells - EDGE + np.arange(EDGE), np.arange(EDGE)] = 1.0
    send_right[: cells - EDGE, EDGE] = r ** (cells - np.arange(cells - EDGE))
    from_left = np.concatenate(
        [both(ov + cells - (cells - EDGE + k)),
         np.concatenate([tail * r**ov, tail * r**ov * (r - 1.0 / r)], axis=-1)],
        axis=0,
    )
    send_left = np.zeros((cells, EDGE + 1))
    send_left[np.arange(EDGE), np.arange(EDGE)] = 1.0
    send_left[EDGE:, EDGE] = r ** (np.arange(EDGE, cells) + 1.0)
    from_right = np.concatenate(
        [both(ov - cells - k),
         np.concatenate([tail * r ** (cells - 1 - ov), tail * r ** (cells - 1 - ov) * (1.0 / r - r)], axis=-1)],
        axis=0,
    )
    return [np.asarray(t, np.float32) for t in (own, send_right, from_left, send_left, from_right)]


def neighbours(value, axis, wrap):
    size = lax.axis_size(axis)
    up = [(i, (i + 1) % size) for i in range(size if wrap else size - 1)]
    down = [(j, i) for i, j in up]
    return up, down


def shards(adjoint, coeff, flux, target_cell, donor_owner, donor_cell):
    fields, rows_x, rows_r, cells_a = adjoint.shape
    loop_span = cells_a * lax.axis_size("az")
    rows = rows_x * rows_r
    own_t, send_right_t, from_left_t, send_left_t, from_right_t = halo_tables(cells_a, loop_span)
    lines = adjoint.reshape(fields * rows, cells_a)

    up, down = neighbours(adjoint, "az", True)
    right_moment = jnp.asarray(send_right_t[:, EDGE])
    left_moment = jnp.asarray(send_left_t[:, EDGE])
    to_right = jnp.concatenate(
        [lines[:, cells_a - EDGE :], jnp.sum(lines * right_moment[None], axis=1, keepdims=True)], axis=1
    ).T
    to_left = jnp.concatenate(
        [lines[:, :EDGE], jnp.sum(lines * left_moment[None], axis=1, keepdims=True)], axis=1
    ).T
    from_left = lax.ppermute(to_right, "az", up)
    from_right = lax.ppermute(to_left, "az", down)
    both = jnp.einsum("lc,co->lo", lines, jnp.asarray(own_t), precision=HI)
    both = both + jnp.einsum("kl,ko->lo", from_left, jnp.asarray(from_left_t), precision=HI)
    both = both + jnp.einsum("kl,ko->lo", from_right, jnp.asarray(from_right_t), precision=HI)
    both = both.reshape(fields, rows_x, rows_r, 2 * cells_a)
    filtered = both[..., :cells_a]
    along_a = both[..., cells_a:]

    row_ids = jnp.arange(rows, dtype=jnp.int32)
    lane_ids = jnp.arange(cells_a, dtype=jnp.int32)
    t_rows = (target_cell[:, None] // cells_a == row_ids[None, :]).astype(jnp.float32)
    t_lanes = (target_cell[:, None] % cells_a == lane_ids[None, :]).astype(jnp.float32)
    flat = filtered.reshape(fields, rows, cells_a)
    picked = jnp.einsum("tk,fka->fta", t_rows, flat, precision=HI)
    source = sat_gain * jnp.sum(picked * t_lanes[None], axis=2)

    owner_rows = donor_owner[:, 0]
    owners = lax.axis_size("gx")
    capacity = target_cell.shape[0] // 8
    onehot = (owner_rows[:, None] == jnp.arange(owners, dtype=jnp.int32)[None, :]).astype(jnp.int32)
    slot_rank = jnp.sum(onehot * (jnp.cumsum(onehot, axis=0) - 1), axis=1)
    slot_place = owner_rows * capacity + slot_rank
    packed = jnp.concatenate([source, donor_cell.astype(jnp.float32)[None, :]], axis=0)
    by_rank = (slot_rank[None, :] == jnp.arange(capacity, dtype=jnp.int32)[:, None]).astype(jnp.float32)
    spread_out = (packed[:, None, :] * by_rank[None]).reshape((fields + 1) * capacity, -1)
    outbox = jnp.einsum("qt,to->oq", spread_out, onehot.astype(jnp.float32), precision=HI)
    received = lax.all_to_all(outbox, "gx", split_axis=0, concat_axis=0, tiled=True)
    taken = jnp.einsum("nk,fna->fka", t_rows, -source[:, :, None] * t_lanes[None], precision=HI)
    up_x, down_x = neighbours(filtered, "gx", False)
    last_x, first_x, last_r, first_r = filtered[:, -1], filtered[:, 0], filtered[:, :, -1], filtered[:, :, 0]
    before_x = lax.ppermute(last_x, "gx", up_x)[:, None]
    after_x = lax.ppermute(first_x, "gx", down_x)[:, None]
    if lax.axis_size("row") == 2:
        band = lax.axis_index("row")
        other = lax.ppermute(jnp.where(band == 0, last_r, first_r), "row", [(0, 1), (1, 0)])
        before_r = jnp.where(band == 1, other, 0.0)[:, :, None]
        after_r = jnp.where(band == 0, other, 0.0)[:, :, None]
    else:
        up_r, down_r = neighbours(filtered, "row", False)
        before_r = lax.ppermute(last_r, "row", up_r)[:, :, None]
        after_r = lax.ppermute(first_r, "row", down_r)[:, :, None]
    along_x = jnp.concatenate([filtered[:, 1:], after_x], axis=1) - jnp.concatenate(
        [before_x, filtered[:, :-1]], axis=1
    )
    along_r = jnp.concatenate([filtered[:, :, 1:], after_r], axis=2) - jnp.concatenate(
        [before_r, filtered[:, :, :-1]], axis=2
    )
    changes = lax.optimization_barrier((along_x, along_r, along_a))
    gradient = filtered + taken.reshape(adjoint.shape)
    for direction, change in enumerate(changes):
        mixing = flux[direction, 0][:, None, None, None] * change[0][None]
        for f in range(1, fields):
            mixing = mixing + flux[direction, f][:, None, None, None] * change[f][None]
        gradient = gradient + coeff[direction][None] * mixing
    gradient, received = lax.optimization_barrier((gradient, received))

    received = received.reshape(owners, fields + 1, capacity).transpose(1, 0, 2).reshape(fields + 1, owners * capacity)
    got_cell = received[fields].astype(jnp.int32)
    d_rows = (got_cell[:, None] // cells_a == row_ids[None, :]).astype(jnp.float32)
    d_lanes = (got_cell[:, None] % cells_a == lane_ids[None, :]).astype(jnp.float32)
    spread = received[:fields, :, None] * d_lanes[None]
    update = jnp.einsum("nk,fna->fka", d_rows, spread, precision=HI)
    return gradient + update.reshape(adjoint.shape)


def solution(mesh):
    return jax.shard_map(
        shards,
        mesh=mesh,
        in_specs=(
            P(None, "gx", "row", "az"),
            P(None, "gx", "row", "az"),
            P(),
            P(("gx", "az", "row")),
            P(("gx", "az", "row"), None),
            P(("gx", "az", "row")),
        ),
        out_specs=P(None, "gx", "row", "az"),
        check_vma=False,
    )
```

```python
import jax
import jax.numpy as jnp
import numpy as np
from jax import lax
from jax.sharding import PartitionSpec as P

filter_alpha = 0.49
sat_gain = 0.5
pade_coeffs = [
    (193.0 + 126.0 * filter_alpha) / 256.0,
    (105.0 + 302.0 * filter_alpha) / 256.0,
    15.0 * (2.0 * filter_alpha - 1.0) / 64.0,
    45.0 * (1.0 - 2.0 * filter_alpha) / 512.0,
    5.0 * (2.0 * filter_alpha - 1.0) / 256.0,
    (1.0 - 2.0 * filter_alpha) / 512.0,
]
HI = lax.Precision.HIGH


root_value = (-1.0 + (1.0 - 4.0 * filter_alpha * filter_alpha) ** 0.5) / (2.0 * filter_alpha)
green_scale = 1.0 / (1.0 + 2.0 * filter_alpha * root_value)
EDGE = 7


def stencil_weight(shift):
    return pade_coeffs[0] if shift == 0 else 0.5 * pade_coeffs[abs(shift)]


def loop_weight(offset, length):
    total = np.zeros(np.shape(offset))
    for shift in range(-5, 6):
        n = np.mod(offset - shift, length)
        images = root_value ** n + root_value ** (length - n)
        total = total + stencil_weight(shift) * green_scale * images / (1.0 - root_value**length)
    return total


def halo_tables(cells, length):
    r = root_value
    tail = green_scale / (1.0 - r**length) * sum(stencil_weight(s) * r ** (-s) for s in range(-5, 6))
    c = np.arange(cells)[:, None]
    o = np.arange(cells)[None, :]

    def both(distance):
        return np.concatenate(
            [loop_weight(distance, length), loop_weight(distance + 1, length) - loop_weight(distance - 1, length)],
            axis=-1,
        )

    own = both(o - c)
    k = np.arange(EDGE)[:, None]
    ov = np.arange(cells)[None, :]
    send_right = np.zeros((cells, EDGE + 1))
    send_right[cells - EDGE + np.arange(EDGE), np.arange(EDGE)] = 1.0
    send_right[: cells - EDGE, EDGE] = r ** (cells - np.arange(cells - EDGE))
    from_left = np.concatenate(
        [both(ov + cells - (cells - EDGE + k)),
         np.concatenate([tail * r**ov, tail * r**ov * (r - 1.0 / r)], axis=-1)],
        axis=0,
    )
    send_left = np.zeros((cells, EDGE + 1))
    send_left[np.arange(EDGE), np.arange(EDGE)] = 1.0
    send_left[EDGE:, EDGE] = r ** (np.arange(EDGE, cells) + 1.0)
    from_right = np.concatenate(
        [both(ov - cells - k),
         np.concatenate([tail * r ** (cells - 1 - ov), tail * r ** (cells - 1 - ov) * (1.0 / r - r)], axis=-1)],
        axis=0,
    )
    return [np.asarray(t, np.float32) for t in (own, send_right, from_left, send_left, from_right)]


def neighbours(value, axis, wrap):
    size = lax.axis_size(axis)
    up = [(i, (i + 1) % size) for i in range(size if wrap else size - 1)]
    down = [(j, i) for i, j in up]
    return up, down


def shards(adjoint, coeff, flux, target_cell, donor_owner, donor_cell):
    fields, rows_x, rows_r, cells_a = adjoint.shape
    loop_span = cells_a * lax.axis_size("az")
    rows = rows_x * rows_r
    own_t, send_right_t, from_left_t, send_left_t, from_right_t = halo_tables(cells_a, loop_span)
    lines = adjoint.reshape(fields * rows, cells_a)

    up, down = neighbours(adjoint, "az", True)
    right_moment = jnp.asarray(send_right_t[:, EDGE])
    left_moment = jnp.asarray(send_left_t[:, EDGE])
    to_right = jnp.concatenate(
        [lines[:, cells_a - EDGE :], jnp.sum(lines * right_moment[None], axis=1, keepdims=True)], axis=1
    ).T
    to_left = jnp.concatenate(
        [lines[:, :EDGE], jnp.sum(lines * left_moment[None], axis=1, keepdims=True)], axis=1
    ).T
    from_left = lax.ppermute(to_right, "az", up)
    from_right = lax.ppermute(to_left, "az", down)
    both = jnp.einsum("lc,co->lo", lines, jnp.asarray(own_t), precision=HI)
    both = both + jnp.einsum("kl,ko->lo", from_left, jnp.asarray(from_left_t), precision=HI)
    both = both + jnp.einsum("kl,ko->lo", from_right, jnp.asarray(from_right_t), precision=HI)
    both = both.reshape(fields, rows_x, rows_r, 2 * cells_a)
    filtered = both[..., :cells_a]
    along_a = both[..., cells_a:]

    row_ids = jnp.arange(rows, dtype=jnp.int32)
    lane_ids = jnp.arange(cells_a, dtype=jnp.int32)
    t_rows = (target_cell[:, None] // cells_a == row_ids[None, :]).astype(jnp.float32)
    t_lanes = (target_cell[:, None] % cells_a == lane_ids[None, :]).astype(jnp.float32)
    flat = filtered.reshape(fields, rows, cells_a)
    picked = jnp.einsum("tk,fka->fta", t_rows, flat, precision=HI)
    source = sat_gain * jnp.sum(picked * t_lanes[None], axis=2)

    owner_rows = donor_owner[:, 0]
    owners = lax.axis_size("gx")
    capacity = target_cell.shape[0] // 8
    onehot = (owner_rows[:, None] == jnp.arange(owners, dtype=jnp.int32)[None, :]).astype(jnp.int32)
    slot_rank = jnp.sum(onehot * (jnp.cumsum(onehot, axis=0) - 1), axis=1)
    slot_place = owner_rows * capacity + slot_rank
    packed = jnp.concatenate([source, donor_cell.astype(jnp.float32)[None, :]], axis=0)
    by_rank = (slot_rank[None, :] == jnp.arange(capacity, dtype=jnp.int32)[:, None]).astype(jnp.float32)
    spread_out = (packed[:, None, :] * by_rank[None]).reshape((fields + 1) * capacity, -1)
    if owners & (owners - 1) == 0:
        ahead = (owner_rows - lax.axis_index("gx")) % owners
        rotated = (ahead[:, None] == jnp.arange(owners, dtype=jnp.int32)[None, :]).astype(jnp.float32)
        received = jnp.einsum("qt,to->oq", spread_out, rotated, precision=HI)
        width = received.shape[1]
        step = 1
        while step < owners:
            view = received.reshape(owners // (2 * step), 2, step, width)
            moved = lax.ppermute(
                view[:, 1], "gx", [(i, (i + step) % owners) for i in range(owners)]
            )
            received = view.at[:, 1].set(moved).reshape(owners, width)
            step *= 2
    else:
        outbox = jnp.einsum("qt,to->oq", spread_out, onehot.astype(jnp.float32), precision=HI)
        received = lax.all_to_all(outbox, "gx", split_axis=0, concat_axis=0, tiled=True)
    taken = jnp.einsum("nk,fna->fka", t_rows, -source[:, :, None] * t_lanes[None], precision=HI)
    up_x, down_x = neighbours(filtered, "gx", False)
    last_x, first_x, last_r, first_r = filtered[:, -1], filtered[:, 0], filtered[:, :, -1], filtered[:, :, 0]
    before_x = lax.ppermute(last_x, "gx", up_x)[:, None]
    after_x = lax.ppermute(first_x, "gx", down_x)[:, None]
    if lax.axis_size("row") == 2:
        band = lax.axis_index("row")
        other = lax.ppermute(jnp.where(band == 0, last_r, first_r), "row", [(0, 1), (1, 0)])
        before_r = jnp.where(band == 1, other, 0.0)[:, :, None]
        after_r = jnp.where(band == 0, other, 0.0)[:, :, None]
    else:
        up_r, down_r = neighbours(filtered, "row", False)
        before_r = lax.ppermute(last_r, "row", up_r)[:, :, None]
        after_r = lax.ppermute(first_r, "row", down_r)[:, :, None]
    along_x = jnp.concatenate([filtered[:, 1:], after_x], axis=1) - jnp.concatenate(
        [before_x, filtered[:, :-1]], axis=1
    )
    along_r = jnp.concatenate([filtered[:, :, 1:], after_r], axis=2) - jnp.concatenate(
        [before_r, filtered[:, :, :-1]], axis=2
    )
    changes = lax.optimization_barrier((along_x, along_r, along_a))
    gradient = filtered + taken.reshape(adjoint.shape)
    for direction, change in enumerate(changes):
        mixing = flux[direction, 0][:, None, None, None] * change[0][None]
        for f in range(1, fields):
            mixing = mixing + flux[direction, f][:, None, None, None] * change[f][None]
        gradient = gradient + coeff[direction][None] * mixing
    gradient, received = lax.optimization_barrier((gradient, received))

    received = received.reshape(owners, fields + 1, capacity).transpose(1, 0, 2).reshape(fields + 1, owners * capacity)
    got_cell = received[fields].astype(jnp.int32)
    d_rows = (got_cell[:, None] // cells_a == row_ids[None, :]).astype(jnp.float32)
    d_lanes = (got_cell[:, None] % cells_a == lane_ids[None, :]).astype(jnp.float32)
    spread = received[:fields, :, None] * d_lanes[None]
    update = jnp.einsum("nk,fna->fka", d_rows, spread, precision=HI)
    return gradient + update.reshape(adjoint.shape)


def solution(mesh):
    return jax.shard_map(
        shards,
        mesh=mesh,
        in_specs=(
            P(None, "gx", "row", "az"),
            P(None, "gx", "row", "az"),
            P(),
            P(("gx", "az", "row")),
            P(("gx", "az", "row"), None),
            P(("gx", "az", "row")),
        ),
        out_specs=P(None, "gx", "row", "az"),
        check_vma=False,
    )
```

```python
import jax
import jax.numpy as jnp
import numpy as np
from jax import lax
from jax.sharding import PartitionSpec as P

filter_alpha = 0.49
sat_gain = 0.5
pade_coeffs = [
    (193.0 + 126.0 * filter_alpha) / 256.0,
    (105.0 + 302.0 * filter_alpha) / 256.0,
    15.0 * (2.0 * filter_alpha - 1.0) / 64.0,
    45.0 * (1.0 - 2.0 * filter_alpha) / 512.0,
    5.0 * (2.0 * filter_alpha - 1.0) / 256.0,
    (1.0 - 2.0 * filter_alpha) / 512.0,
]
HI = lax.Precision.HIGH


root_value = (-1.0 + (1.0 - 4.0 * filter_alpha * filter_alpha) ** 0.5) / (2.0 * filter_alpha)
green_scale = 1.0 / (1.0 + 2.0 * filter_alpha * root_value)
EDGE = 7


def stencil_weight(shift):
    return pade_coeffs[0] if shift == 0 else 0.5 * pade_coeffs[abs(shift)]


def loop_weight(offset, length):
    total = np.zeros(np.shape(offset))
    for shift in range(-5, 6):
        n = np.mod(offset - shift, length)
        images = root_value ** n + root_value ** (length - n)
        total = total + stencil_weight(shift) * green_scale * images / (1.0 - root_value**length)
    return total


def halo_tables(cells, length):
    r = root_value
    tail = green_scale / (1.0 - r**length) * sum(stencil_weight(s) * r ** (-s) for s in range(-5, 6))
    c = np.arange(cells)[:, None]
    o = np.arange(cells)[None, :]

    def both(distance):
        return np.concatenate(
            [loop_weight(distance, length), loop_weight(distance + 1, length) - loop_weight(distance - 1, length)],
            axis=-1,
        )

    own = both(o - c)
    k = np.arange(EDGE)[:, None]
    ov = np.arange(cells)[None, :]
    send_right = np.zeros((cells, EDGE + 1))
    send_right[cells - EDGE + np.arange(EDGE), np.arange(EDGE)] = 1.0
    send_right[: cells - EDGE, EDGE] = r ** (cells - np.arange(cells - EDGE))
    from_left = np.concatenate(
        [both(ov + cells - (cells - EDGE + k)),
         np.concatenate([tail * r**ov, tail * r**ov * (r - 1.0 / r)], axis=-1)],
        axis=0,
    )
    send_left = np.zeros((cells, EDGE + 1))
    send_left[np.arange(EDGE), np.arange(EDGE)] = 1.0
    send_left[EDGE:, EDGE] = r ** (np.arange(EDGE, cells) + 1.0)
    from_right = np.concatenate(
        [both(ov - cells - k),
         np.concatenate([tail * r ** (cells - 1 - ov), tail * r ** (cells - 1 - ov) * (1.0 / r - r)], axis=-1)],
        axis=0,
    )
    return [np.asarray(t, np.float32) for t in (own, send_right, from_left, send_left, from_right)]


def neighbours(value, axis, wrap):
    size = lax.axis_size(axis)
    up = [(i, (i + 1) % size) for i in range(size if wrap else size - 1)]
    down = [(j, i) for i, j in up]
    return up, down


def shards(adjoint, coeff, flux, target_cell, donor_owner, donor_cell):
    fields, rows_x, rows_r, cells_a = adjoint.shape
    loop_span = cells_a * lax.axis_size("az")
    rows = rows_x * rows_r
    own_t, send_right_t, from_left_t, send_left_t, from_right_t = halo_tables(cells_a, loop_span)
    lines = adjoint.reshape(fields * rows, cells_a)

    up, down = neighbours(adjoint, "az", True)
    right_moment = jnp.asarray(send_right_t[:, EDGE])
    left_moment = jnp.asarray(send_left_t[:, EDGE])
    to_right = jnp.concatenate(
        [lines[:, cells_a - EDGE :], jnp.sum(lines * right_moment[None], axis=1, keepdims=True)], axis=1
    ).T
    to_left = jnp.concatenate(
        [lines[:, :EDGE], jnp.sum(lines * left_moment[None], axis=1, keepdims=True)], axis=1
    ).T
    from_left = lax.ppermute(to_right, "az", up)
    from_right = lax.ppermute(to_left, "az", down)
    both = jnp.einsum("lc,co->lo", lines, jnp.asarray(own_t), precision=HI)
    both = both + jnp.einsum("kl,ko->lo", from_left, jnp.asarray(from_left_t), precision=HI)
    both = both + jnp.einsum("kl,ko->lo", from_right, jnp.asarray(from_right_t), precision=HI)
    both = both.reshape(fields, rows_x, rows_r, 2 * cells_a)
    filtered = both[..., :cells_a]
    along_a = both[..., cells_a:]

    row_ids = jnp.arange(rows, dtype=jnp.int32)
    lane_ids = jnp.arange(cells_a, dtype=jnp.int32)
    t_rows = (target_cell[:, None] // cells_a == row_ids[None, :]).astype(jnp.float32)
    t_lanes = (target_cell[:, None] % cells_a == lane_ids[None, :]).astype(jnp.float32)
    flat = filtered.reshape(fields, rows, cells_a)
    picked = jnp.einsum("tk,fka->fta", t_rows, flat, precision=HI)
    source = sat_gain * jnp.sum(picked * t_lanes[None], axis=2)

    owner_rows = donor_owner[:, 0]
    owners = lax.axis_size("gx")
    capacity = target_cell.shape[0] // 8
    onehot = (owner_rows[:, None] == jnp.arange(owners, dtype=jnp.int32)[None, :]).astype(jnp.int32)
    slot_rank = jnp.sum(onehot * (jnp.cumsum(onehot, axis=0) - 1), axis=1)
    slot_place = owner_rows * capacity + slot_rank
    packed = jnp.concatenate([source, donor_cell.astype(jnp.float32)[None, :]], axis=0)
    by_rank = (slot_rank[None, :] == jnp.arange(capacity, dtype=jnp.int32)[:, None]).astype(jnp.float32)
    spread_out = (packed[:, None, :] * by_rank[None]).reshape((fields + 1) * capacity, -1)
    outbox = jnp.einsum("qt,to->oq", spread_out, onehot.astype(jnp.float32), precision=HI)
    received = lax.all_to_all(outbox, "gx", split_axis=0, concat_axis=0, tiled=True)
    taken = jnp.einsum("nk,fna->fka", t_rows, -source[:, :, None] * t_lanes[None], precision=HI)
    up_x, down_x = neighbours(filtered, "gx", False)
    last_x, first_x, last_r, first_r = filtered[:, -1], filtered[:, 0], filtered[:, :, -1], filtered[:, :, 0]
    before_x = lax.ppermute(last_x, "gx", up_x)[:, None]
    after_x = lax.ppermute(first_x, "gx", down_x)[:, None]
    if lax.axis_size("row") == 2:
        band = lax.axis_index("row")
        other = lax.ppermute(jnp.where(band == 0, last_r, first_r), "row", [(0, 1), (1, 0)])
        before_r = jnp.where(band == 1, other, 0.0)[:, :, None]
        after_r = jnp.where(band == 0, other, 0.0)[:, :, None]
    else:
        up_r, down_r = neighbours(filtered, "row", False)
        before_r = lax.ppermute(last_r, "row", up_r)[:, :, None]
        after_r = lax.ppermute(first_r, "row", down_r)[:, :, None]
    along_x = jnp.concatenate([filtered[:, 1:], after_x], axis=1) - jnp.concatenate(
        [before_x, filtered[:, :-1]], axis=1
    )
    along_r = jnp.concatenate([filtered[:, :, 1:], after_r], axis=2) - jnp.concatenate(
        [before_r, filtered[:, :, :-1]], axis=2
    )
    changes = lax.optimization_barrier((along_x, along_r, along_a))
    gradient = filtered + taken.reshape(adjoint.shape)
    for direction, change in enumerate(changes):
        mixing = flux[direction, 0][:, None, None, None] * change[0][None]
        for f in range(1, fields):
            mixing = mixing + flux[direction, f][:, None, None, None] * change[f][None]
        gradient = gradient + coeff[direction][None] * mixing
    gradient, received = lax.optimization_barrier((gradient, received))

    received = received.reshape(owners, fields + 1, capacity).transpose(1, 0, 2).reshape(fields + 1, owners * capacity)
    got_cell = received[fields].astype(jnp.int32)
    d_rows = (got_cell[:, None] // cells_a == row_ids[None, :]).astype(jnp.float32)
    d_lanes = (got_cell[:, None] % cells_a == lane_ids[None, :]).astype(jnp.float32)
    weighted = (received[:fields, None, :] * d_rows.T[None]).reshape(fields * rows, -1)
    update = jnp.dot(weighted, d_lanes, precision=HI)
    return gradient + update.reshape(adjoint.shape)


def solution(mesh):
    return jax.shard_map(
        shards,
        mesh=mesh,
        in_specs=(
            P(None, "gx", "row", "az"),
            P(None, "gx", "row", "az"),
            P(),
            P(("gx", "az", "row")),
            P(("gx", "az", "row"), None),
            P(("gx", "az", "row")),
        ),
        out_specs=P(None, "gx", "row", "az"),
        check_vma=False,
    )
```

```python
import jax
import jax.numpy as jnp
import numpy as np
from jax import lax
from jax.sharding import PartitionSpec as P

filter_alpha = 0.49
sat_gain = 0.5
pade_coeffs = [
    (193.0 + 126.0 * filter_alpha) / 256.0,
    (105.0 + 302.0 * filter_alpha) / 256.0,
    15.0 * (2.0 * filter_alpha - 1.0) / 64.0,
    45.0 * (1.0 - 2.0 * filter_alpha) / 512.0,
    5.0 * (2.0 * filter_alpha - 1.0) / 256.0,
    (1.0 - 2.0 * filter_alpha) / 512.0,
]
HI = lax.Precision.HIGH


root_value = (-1.0 + (1.0 - 4.0 * filter_alpha * filter_alpha) ** 0.5) / (2.0 * filter_alpha)
green_scale = 1.0 / (1.0 + 2.0 * filter_alpha * root_value)
EDGE = 7


def stencil_weight(shift):
    return pade_coeffs[0] if shift == 0 else 0.5 * pade_coeffs[abs(shift)]


def loop_weight(offset, length):
    total = np.zeros(np.shape(offset))
    for shift in range(-5, 6):
        n = np.mod(offset - shift, length)
        images = root_value ** n + root_value ** (length - n)
        total = total + stencil_weight(shift) * green_scale * images / (1.0 - root_value**length)
    return total


def halo_tables(cells, length):
    r = root_value
    tail = green_scale / (1.0 - r**length) * sum(stencil_weight(s) * r ** (-s) for s in range(-5, 6))
    c = np.arange(cells)[:, None]
    o = np.arange(cells)[None, :]

    def both(distance):
        return np.concatenate(
            [loop_weight(distance, length), loop_weight(distance + 1, length) - loop_weight(distance - 1, length)],
            axis=-1,
        )

    own = both(o - c)
    k = np.arange(EDGE)[:, None]
    ov = np.arange(cells)[None, :]
    send_right = np.zeros((cells, EDGE + 1))
    send_right[cells - EDGE + np.arange(EDGE), np.arange(EDGE)] = 1.0
    send_right[: cells - EDGE, EDGE] = r ** (cells - np.arange(cells - EDGE))
    from_left = np.concatenate(
        [both(ov + cells - (cells - EDGE + k)),
         np.concatenate([tail * r**ov, tail * r**ov * (r - 1.0 / r)], axis=-1)],
        axis=0,
    )
    send_left = np.zeros((cells, EDGE + 1))
    send_left[np.arange(EDGE), np.arange(EDGE)] = 1.0
    send_left[EDGE:, EDGE] = r ** (np.arange(EDGE, cells) + 1.0)
    from_right = np.concatenate(
        [both(ov - cells - k),
         np.concatenate([tail * r ** (cells - 1 - ov), tail * r ** (cells - 1 - ov) * (1.0 / r - r)], axis=-1)],
        axis=0,
    )
    return [np.asarray(t, np.float32) for t in (own, send_right, from_left, send_left, from_right)]


def neighbours(value, axis, wrap):
    size = lax.axis_size(axis)
    up = [(i, (i + 1) % size) for i in range(size if wrap else size - 1)]
    down = [(j, i) for i, j in up]
    return up, down


def shards(adjoint, coeff, flux, target_cell, donor_owner, donor_cell):
    fields, rows_x, rows_r, cells_a = adjoint.shape
    loop_span = cells_a * lax.axis_size("az")
    rows = rows_x * rows_r
    own_t, send_right_t, from_left_t, send_left_t, from_right_t = halo_tables(cells_a, loop_span)
    lines = adjoint.reshape(fields * rows, cells_a)

    up, down = neighbours(adjoint, "az", True)
    right_moment = jnp.asarray(send_right_t[:, EDGE])
    left_moment = jnp.asarray(send_left_t[:, EDGE])
    to_right = jnp.concatenate(
        [lines[:, cells_a - EDGE :], jnp.sum(lines * right_moment[None], axis=1, keepdims=True)], axis=1
    ).T
    to_left = jnp.concatenate(
        [lines[:, :EDGE], jnp.sum(lines * left_moment[None], axis=1, keepdims=True)], axis=1
    ).T
    from_left = lax.ppermute(to_right, "az", up)
    from_right = lax.ppermute(to_left, "az", down)
    both = jnp.einsum("lc,co->lo", lines, jnp.asarray(own_t), precision=HI)
    both = both + jnp.einsum("kl,ko->lo", from_left, jnp.asarray(from_left_t), precision=HI)
    both = both + jnp.einsum("kl,ko->lo", from_right, jnp.asarray(from_right_t), precision=HI)
    both = both.reshape(fields, rows_x, rows_r, 2 * cells_a)
    filtered = both[..., :cells_a]
    along_a = both[..., cells_a:]

    row_ids = jnp.arange(rows, dtype=jnp.int32)
    lane_ids = jnp.arange(cells_a, dtype=jnp.int32)
    t_rows = (target_cell[:, None] // cells_a == row_ids[None, :]).astype(jnp.float32)
    t_lanes = (target_cell[:, None] % cells_a == lane_ids[None, :]).astype(jnp.float32)
    flat = filtered.reshape(fields * rows, cells_a)
    by_lane = jnp.einsum("la,ta->lt", flat, t_lanes, precision=HI).reshape(fields, rows, -1)
    source = sat_gain * jnp.sum(by_lane * t_rows.T[None], axis=1)

    owner_rows = donor_owner[:, 0]
    owners = lax.axis_size("gx")
    capacity = target_cell.shape[0] // 8
    onehot = (owner_rows[:, None] == jnp.arange(owners, dtype=jnp.int32)[None, :]).astype(jnp.int32)
    slot_rank = jnp.sum(onehot * (jnp.cumsum(onehot, axis=0) - 1), axis=1)
    slot_place = owner_rows * capacity + slot_rank
    packed = jnp.concatenate([source, donor_cell.astype(jnp.float32)[None, :]], axis=0)
    by_rank = (slot_rank[None, :] == jnp.arange(capacity, dtype=jnp.int32)[:, None]).astype(jnp.float32)
    spread_out = (packed[:, None, :] * by_rank[None]).reshape((fields + 1) * capacity, -1)
    outbox = jnp.einsum("qt,to->oq", spread_out, onehot.astype(jnp.float32), precision=HI)
    received = lax.all_to_all(outbox, "gx", split_axis=0, concat_axis=0, tiled=True)
    taken = jnp.einsum("nk,fna->fka", t_rows, -source[:, :, None] * t_lanes[None], precision=HI)
    up_x, down_x = neighbours(filtered, "gx", False)
    last_x, first_x, last_r, first_r = filtered[:, -1], filtered[:, 0], filtered[:, :, -1], filtered[:, :, 0]
    before_x = lax.ppermute(last_x, "gx", up_x)[:, None]
    after_x = lax.ppermute(first_x, "gx", down_x)[:, None]
    if lax.axis_size("row") == 2:
        band = lax.axis_index("row")
        other = lax.ppermute(jnp.where(band == 0, last_r, first_r), "row", [(0, 1), (1, 0)])
        before_r = jnp.where(band == 1, other, 0.0)[:, :, None]
        after_r = jnp.where(band == 0, other, 0.0)[:, :, None]
    else:
        up_r, down_r = neighbours(filtered, "row", False)
        before_r = lax.ppermute(last_r, "row", up_r)[:, :, None]
        after_r = lax.ppermute(first_r, "row", down_r)[:, :, None]
    along_x = jnp.concatenate([filtered[:, 1:], after_x], axis=1) - jnp.concatenate(
        [before_x, filtered[:, :-1]], axis=1
    )
    along_r = jnp.concatenate([filtered[:, :, 1:], after_r], axis=2) - jnp.concatenate(
        [before_r, filtered[:, :, :-1]], axis=2
    )
    changes = lax.optimization_barrier((along_x, along_r, along_a))
    gradient = filtered + taken.reshape(adjoint.shape)
    for direction, change in enumerate(changes):
        mixing = flux[direction, 0][:, None, None, None] * change[0][None]
        for f in range(1, fields):
            mixing = mixing + flux[direction, f][:, None, None, None] * change[f][None]
        gradient = gradient + coeff[direction][None] * mixing
    gradient, received = lax.optimization_barrier((gradient, received))

    received = received.reshape(owners, fields + 1, capacity).transpose(1, 0, 2).reshape(fields + 1, owners * capacity)
    got_cell = received[fields].astype(jnp.int32)
    d_rows = (got_cell[:, None] // cells_a == row_ids[None, :]).astype(jnp.float32)
    d_lanes = (got_cell[:, None] % cells_a == lane_ids[None, :]).astype(jnp.float32)
    weighted = (received[:fields, None, :] * d_rows.T[None]).reshape(fields * rows, -1)
    update = jnp.dot(weighted, d_lanes, precision=HI)
    return gradient + update.reshape(adjoint.shape)


def solution(mesh):
    return jax.shard_map(
        shards,
        mesh=mesh,
        in_specs=(
            P(None, "gx", "row", "az"),
            P(None, "gx", "row", "az"),
            P(),
            P(("gx", "az", "row")),
            P(("gx", "az", "row"), None),
            P(("gx", "az", "row")),
        ),
        out_specs=P(None, "gx", "row", "az"),
        check_vma=False,
    )
```

```python
import jax
import jax.numpy as jnp
import numpy as np
from jax import lax
from jax.sharding import PartitionSpec as P

filter_alpha = 0.49
sat_gain = 0.5
pade_coeffs = [
    (193.0 + 126.0 * filter_alpha) / 256.0,
    (105.0 + 302.0 * filter_alpha) / 256.0,
    15.0 * (2.0 * filter_alpha - 1.0) / 64.0,
    45.0 * (1.0 - 2.0 * filter_alpha) / 512.0,
    5.0 * (2.0 * filter_alpha - 1.0) / 256.0,
    (1.0 - 2.0 * filter_alpha) / 512.0,
]
HI = lax.Precision.HIGH


root_value = (-1.0 + (1.0 - 4.0 * filter_alpha * filter_alpha) ** 0.5) / (2.0 * filter_alpha)
green_scale = 1.0 / (1.0 + 2.0 * filter_alpha * root_value)
EDGE = 7


def stencil_weight(shift):
    return pade_coeffs[0] if shift == 0 else 0.5 * pade_coeffs[abs(shift)]


def loop_weight(offset, length):
    total = np.zeros(np.shape(offset))
    for shift in range(-5, 6):
        n = np.mod(offset - shift, length)
        images = root_value ** n + root_value ** (length - n)
        total = total + stencil_weight(shift) * green_scale * images / (1.0 - root_value**length)
    return total


def halo_tables(cells, length):
    r = root_value
    tail = green_scale / (1.0 - r**length) * sum(stencil_weight(s) * r ** (-s) for s in range(-5, 6))
    c = np.arange(cells)[:, None]
    o = np.arange(cells)[None, :]

    def both(distance):
        return np.concatenate(
            [loop_weight(distance, length), loop_weight(distance + 1, length) - loop_weight(distance - 1, length)],
            axis=-1,
        )

    own = both(o - c)
    k = np.arange(EDGE)[:, None]
    ov = np.arange(cells)[None, :]
    send_right = np.zeros((cells, EDGE + 1))
    send_right[cells - EDGE + np.arange(EDGE), np.arange(EDGE)] = 1.0
    send_right[: cells - EDGE, EDGE] = r ** (cells - np.arange(cells - EDGE))
    from_left = np.concatenate(
        [both(ov + cells - (cells - EDGE + k)),
         np.concatenate([tail * r**ov, tail * r**ov * (r - 1.0 / r)], axis=-1)],
        axis=0,
    )
    send_left = np.zeros((cells, EDGE + 1))
    send_left[np.arange(EDGE), np.arange(EDGE)] = 1.0
    send_left[EDGE:, EDGE] = r ** (np.arange(EDGE, cells) + 1.0)
    from_right = np.concatenate(
        [both(ov - cells - k),
         np.concatenate([tail * r ** (cells - 1 - ov), tail * r ** (cells - 1 - ov) * (1.0 / r - r)], axis=-1)],
        axis=0,
    )
    return [np.asarray(t, np.float32) for t in (own, send_right, from_left, send_left, from_right)]


def neighbours(value, axis, wrap):
    size = lax.axis_size(axis)
    up = [(i, (i + 1) % size) for i in range(size if wrap else size - 1)]
    down = [(j, i) for i, j in up]
    return up, down


def shards(adjoint, coeff, flux, target_cell, donor_owner, donor_cell):
    fields, rows_x, rows_r, cells_a = adjoint.shape
    loop_span = cells_a * lax.axis_size("az")
    rows = rows_x * rows_r
    own_t, send_right_t, from_left_t, send_left_t, from_right_t = halo_tables(cells_a, loop_span)
    lines = adjoint.reshape(fields * rows, cells_a)

    up, down = neighbours(adjoint, "az", True)
    right_moment = jnp.asarray(send_right_t[:, EDGE])
    left_moment = jnp.asarray(send_left_t[:, EDGE])
    to_right = jnp.concatenate(
        [lines[:, cells_a - EDGE :], jnp.sum(lines * right_moment[None], axis=1, keepdims=True)], axis=1
    ).T
    to_left = jnp.concatenate(
        [lines[:, :EDGE], jnp.sum(lines * left_moment[None], axis=1, keepdims=True)], axis=1
    ).T
    from_left = lax.ppermute(to_right, "az", up)
    from_right = lax.ppermute(to_left, "az", down)
    both = jnp.einsum("lc,co->lo", lines, jnp.asarray(own_t), precision=HI)
    both = both + jnp.einsum("kl,ko->lo", from_left, jnp.asarray(from_left_t), precision=HI)
    both = both + jnp.einsum("kl,ko->lo", from_right, jnp.asarray(from_right_t), precision=HI)
    both = both.reshape(fields, rows_x, rows_r, 2 * cells_a)
    filtered = both[..., :cells_a]
    along_a = both[..., cells_a:]

    row_ids = jnp.arange(rows, dtype=jnp.int32)
    lane_ids = jnp.arange(cells_a, dtype=jnp.int32)
    t_rows = (target_cell[:, None] // cells_a == row_ids[None, :]).astype(jnp.float32)
    t_lanes = (target_cell[:, None] % cells_a == lane_ids[None, :]).astype(jnp.float32)
    flat = filtered.reshape(fields * rows, cells_a)
    by_lane = jnp.einsum("la,ta->lt", flat, t_lanes, precision=HI).reshape(fields, rows, -1)
    source = sat_gain * jnp.sum(by_lane * t_rows.T[None], axis=1)

    owner_rows = donor_owner[:, 0]
    owners = lax.axis_size("gx")
    capacity = target_cell.shape[0] // 8
    onehot = (owner_rows[:, None] == jnp.arange(owners, dtype=jnp.int32)[None, :]).astype(jnp.int32)
    slot_rank = jnp.sum(onehot * (jnp.cumsum(onehot, axis=0) - 1), axis=1)
    slot_place = owner_rows * capacity + slot_rank
    packed = jnp.concatenate([source, donor_cell.astype(jnp.float32)[None, :]], axis=0)
    by_rank = (slot_rank[None, :] == jnp.arange(capacity, dtype=jnp.int32)[:, None]).astype(jnp.float32)
    spread_out = (packed[:, None, :] * by_rank[None]).reshape((fields + 1) * capacity, -1)
    outbox = jnp.einsum("qt,to->oq", spread_out, onehot.astype(jnp.float32), precision=HI)
    received = lax.all_to_all(outbox, "gx", split_axis=0, concat_axis=0, tiled=True)
    taken = jnp.dot(
        (-source[:, None, :] * t_rows.T[None]).reshape(fields * rows, -1), t_lanes, precision=HI
    )
    up_x, down_x = neighbours(filtered, "gx", False)
    last_x, first_x, last_r, first_r = filtered[:, -1], filtered[:, 0], filtered[:, :, -1], filtered[:, :, 0]
    before_x = lax.ppermute(last_x, "gx", up_x)[:, None]
    after_x = lax.ppermute(first_x, "gx", down_x)[:, None]
    if lax.axis_size("row") == 2:
        band = lax.axis_index("row")
        other = lax.ppermute(jnp.where(band == 0, last_r, first_r), "row", [(0, 1), (1, 0)])
        before_r = jnp.where(band == 1, other, 0.0)[:, :, None]
        after_r = jnp.where(band == 0, other, 0.0)[:, :, None]
    else:
        up_r, down_r = neighbours(filtered, "row", False)
        before_r = lax.ppermute(last_r, "row", up_r)[:, :, None]
        after_r = lax.ppermute(first_r, "row", down_r)[:, :, None]
    along_x = jnp.concatenate([filtered[:, 1:], after_x], axis=1) - jnp.concatenate(
        [before_x, filtered[:, :-1]], axis=1
    )
    along_r = jnp.concatenate([filtered[:, :, 1:], after_r], axis=2) - jnp.concatenate(
        [before_r, filtered[:, :, :-1]], axis=2
    )
    changes = lax.optimization_barrier((along_x, along_r, along_a))
    gradient = filtered + taken.reshape(adjoint.shape)
    for direction, change in enumerate(changes):
        mixing = flux[direction, 0][:, None, None, None] * change[0][None]
        for f in range(1, fields):
            mixing = mixing + flux[direction, f][:, None, None, None] * change[f][None]
        gradient = gradient + coeff[direction][None] * mixing
    gradient, received = lax.optimization_barrier((gradient, received))

    received = received.reshape(owners, fields + 1, capacity).transpose(1, 0, 2).reshape(fields + 1, owners * capacity)
    got_cell = received[fields].astype(jnp.int32)
    d_rows = (got_cell[:, None] // cells_a == row_ids[None, :]).astype(jnp.float32)
    d_lanes = (got_cell[:, None] % cells_a == lane_ids[None, :]).astype(jnp.float32)
    weighted = (received[:fields, None, :] * d_rows.T[None]).reshape(fields * rows, -1)
    update = jnp.dot(weighted, d_lanes, precision=HI)
    return gradient + update.reshape(adjoint.shape)


def solution(mesh):
    return jax.shard_map(
        shards,
        mesh=mesh,
        in_specs=(
            P(None, "gx", "row", "az"),
            P(None, "gx", "row", "az"),
            P(),
            P(("gx", "az", "row")),
            P(("gx", "az", "row"), None),
            P(("gx", "az", "row")),
        ),
        out_specs=P(None, "gx", "row", "az"),
        check_vma=False,
    )
```
